32 devices in a mesh: clips: 2 (over y), seq: 4 (over z), pair: 4 (over x, core).
Axes of the slice: x: 2, y: 2, z: 4, core: 2. Of those that a mesh axis runs over, the one named last changes fastest.
Arguments:
- queries: bfloat16 [4096, 5120], P(('clips', 'seq', 'pair')), parts along dimension 0, may hold values from -34 to 34
- key_rows: bfloat16 [4096, 5120], P(('clips', 'seq', 'pair')), parts along dimension 0, may hold values from -6 to 6
- value_rows: bfloat16 [4096, 5120], P(('clips', 'seq', 'pair')), parts along dimension 0, may hold values from -6 to 6
- block_lists: int32 [40, 16, 2], replicated, may hold values from 0 to 15, as said below
- block_counts: int32 [40, 16], replicated, may hold values from 1 to 2, as said below
Outputs:
- attended: bfloat16 [4096, 5120], P(('clips', 'seq', 'pair')), parts along dimension 0
The draws below stay inside these ranges and needn't reach their ends.
There are 2 independent parts, one for each index of `clips`. The reference program is written for one: setup_inputs(seed, part) draws one part's arguments, and reference() takes and returns one part's arrays. A program takes and returns all parts, laid end to end along the dimension named above; an argument that names none is the same for every part. Nothing has to cross between parts.
Inputs may be any that keep to these rules, and one draw needn't show every extreme that they name: `block_lists`: for each head and query block the entries are distinct and the first one is the query block itself; entries at positions block_counts[h, b] and beyond are not used. `block_counts`: some query block of some head has exactly 2 live key blocks.
All inputs are finite; a program needn't handle non-finite values.
Results may differ from the reference program's by a relative error of at most 0.0055.
Values may be sent and summed in bfloat16 or wider, within the bound.
No kernel may reach another device: no remote copies, remote signals or barrier semaphores. Data moves between devices by JAX's collectives and lax.ppermute only.
A program may use at most 128 MiB of HBM per device.

```python
import math
import jax
import jax.numpy as jnp
from jax import lax

HEADS = 40
HD = 128
BLOCK = 128
NB = 16
TOKENS = 2048
MAXB = 2


def mask_parts(seed_key):
    base_key = jax.random.fold_in(seed_key, 29)
    head_key = jax.random.fold_in(base_key, 1)
    row_key = jax.random.fold_in(base_key, 2)
    pick_key = jax.random.fold_in(base_key, 3)
    busy_key = jax.random.fold_in(base_key, 4)
    order_key = jax.random.fold_in(base_key, 5)
    lowest = max(1, NB // 50)
    head_base = jax.random.randint(head_key, (HEADS,), lowest, MAXB + 1)
    busiest = jax.random.randint(busy_key, (), 0, HEADS)
    head_base = jnp.where(jnp.arange(HEADS, dtype=jnp.int32) == busiest, MAXB, head_base)
    floor_count = jnp.maximum(1, head_base // 2)
    raw_draw = jax.random.randint(row_key, (HEADS, NB), 0, 1 << 20)
    counts = floor_count[:, None] + raw_draw % (head_base - floor_count + 1)[:, None]
    pick_row = jax.random.randint(pick_key, (HEADS,), 0, NB)
    counts = jnp.where(jnp.arange(NB, dtype=jnp.int32)[None, :] == pick_row[:, None], head_base[:, None], counts)
    ranks = jax.random.randint(order_key, (HEADS, NB, NB), 0, 1 << 16) * NB + jnp.arange(NB, dtype=jnp.int32)[None, None, :]
    diagonal = jnp.arange(NB, dtype=jnp.int32)[:, None] == jnp.arange(NB, dtype=jnp.int32)[None, :]
    ranks = jnp.where(diagonal[None, :, :], (1 << 16) * NB + NB, ranks)
    lists = lax.top_k(ranks, MAXB)[1].astype(jnp.int32)
    return (lists, counts.astype(jnp.int32))


def draw_queries(key, part):
    full_shape = (TOKENS, HEADS * HD)
    sample = jnp.clip(jax.random.normal(jax.random.fold_in(key, 13), full_shape, jnp.float32), -6.0, 6.0)
    return sample.astype(jnp.bfloat16)


def draw_key_rows(key, part):
    full_shape = (TOKENS, HEADS * HD)
    sample = jnp.clip(jax.random.normal(jax.random.fold_in(key, 17), full_shape, jnp.float32), -6.0, 6.0)
    return sample.astype(jnp.bfloat16)


def draw_block_lists(key, part):
    lists, counts = mask_parts(key)
    return lists


def draw_block_counts(key, part):
    lists, counts = mask_parts(key)
    return counts


def shard_levels(rng, extent, cuts, least, largest):
    factor_of = 1.0
    for position, shards_of in cuts:
        steps = jax.random.uniform(jax.random.fold_in(jax.random.fold_in(rng, 6), position), (shards_of,), jnp.float32, least / len(cuts), largest / len(cuts))
        factor_of = factor_of * jnp.repeat(jnp.exp(steps), extent[position] // shards_of).reshape((-1,) + (1,) * (len(extent) - 1 - position))
    return factor_of


def centred(own_key, extent, scale, limit, shards=(), kind=jnp.bfloat16):
    drawn = jax.random.normal(own_key, extent, jnp.float32) * scale
    if len(shards) > 0:
        drawn = shard_levels(own_key, extent, shards, -0.22, 0.18) * drawn
    return jnp.clip(drawn, min=-limit, max=limit).astype(kind)


def setup_inputs(seed: int = 0, part: int = 0) -> dict:
    splits = jax.random.split(jax.random.key(seed), 6)
    part_splits = jax.random.split(jax.random.fold_in(splits[5], part), 6)
    queries = draw_queries(jax.random.fold_in(jax.random.fold_in(splits[5], part), 71), part)
    key_rows = draw_key_rows(jax.random.fold_in(jax.random.fold_in(splits[5], part), 71), part)
    value_rows = centred(part_splits[2], (TOKENS, HEADS * HD), 1.0, 6.0, ((0, 16),))
    block_lists = draw_block_lists(jax.random.fold_in(splits[5], 71), part)
    block_counts = draw_block_counts(jax.random.fold_in(splits[5], 71), part)
    return {"queries": queries, "key_rows": key_rows, "value_rows": value_rows, "block_lists": block_lists, "block_counts": block_counts}


def reference(queries, key_rows, value_rows, block_lists, block_counts):
    score_scale = 1.0 / math.sqrt(HD)

    def one_head(head_id):
        col_start = head_id * HD
        head_query = lax.dynamic_slice_in_dim(queries, col_start, HD, 1).reshape(NB, BLOCK, HD)
        head_key = lax.dynamic_slice_in_dim(key_rows, col_start, HD, 1).reshape(NB, BLOCK, HD)
        head_value = lax.dynamic_slice_in_dim(value_rows, col_start, HD, 1).reshape(NB, BLOCK, HD)
        own_lists = block_lists[head_id]
        own_counts = block_counts[head_id]
        key_gathered = head_key[own_lists]
        value_gathered = head_value[own_lists]
        scores = jnp.einsum('nad,nmbd->namb', head_query.astype(jnp.float32), key_gathered.astype(jnp.float32)) * score_scale
        live_mask = (jnp.arange(MAXB, dtype=jnp.int32)[None, :] < own_counts[:, None])[:, None, :, None]
        row_max = lax.optimization_barrier(jnp.max(jnp.where(live_mask, scores, -jnp.inf), axis=(2, 3), keepdims=True))
        raised = jnp.where(live_mask, jnp.exp(scores - row_max), 0.0)
        total = lax.optimization_barrier(jnp.sum(raised, axis=(2, 3)))
        weights = raised.astype(jnp.bfloat16)
        mixed_out = jnp.einsum('namb,nmbd->nad', weights.astype(jnp.float32), value_gathered.astype(jnp.float32))
        return (mixed_out / total[:, :, None]).astype(jnp.bfloat16)
    heads_out = lax.map(one_head, jnp.arange(HEADS, dtype=jnp.int32))
    return heads_out.transpose(1, 2, 0, 3).reshape(TOKENS, HEADS * HD)
```

```python
import math

import jax
import jax.numpy as jnp
from jax import lax
from jax.sharding import Mesh
from jax.sharding import PartitionSpec as P

HEADS = 40
HD = 128
BLOCK = 128

ROWS = ("clips", "seq", "px", "pc")
GROUP = ("seq", "px")


def body(queries, key_rows, value_rows, block_lists, block_counts):
    seq_count = lax.axis_size("seq")
    px_count = lax.axis_size("px")
    pc_count = lax.axis_size("pc")
    group_count = seq_count * px_count
    group_place = lax.axis_index("seq") * px_count + lax.axis_index("px")
    pc_place = lax.axis_index("pc")
    tok_rows = queries.shape[0]
    local_blocks = tok_rows // BLOCK
    block_total = block_lists.shape[1]
    max_visits = block_lists.shape[2]
    heads_per = -(-HEADS // group_count)
    padded_heads = heads_per * group_count
    score_scale = 1.0 / math.sqrt(HD)

    def to_groups(rows_in):
        widened = rows_in.reshape(tok_rows, HEADS, HD)
        if padded_heads > HEADS:
            widened = jnp.pad(widened, ((0, 0), (0, padded_heads - HEADS), (0, 0)))
        return widened.reshape(tok_rows, group_count, heads_per * HD).transpose(1, 0, 2)

    def exchange(rows_in):
        return lax.all_to_all(to_groups(rows_in), GROUP, 0, 0, tiled=True)

    query_own = exchange(queries)
    key_part = exchange(key_rows)
    value_part = exchange(value_rows)
    key_all = lax.all_gather(key_part, "pc", axis=1)
    value_all = lax.all_gather(value_part, "pc", axis=1)

    own_count = group_count * local_blocks
    query_h = query_own.reshape(own_count, BLOCK, heads_per, HD).transpose(2, 0, 1, 3)
    key_h = key_all.reshape(block_total, BLOCK, heads_per, HD).transpose(2, 0, 1, 3)
    value_h = value_all.reshape(block_total, BLOCK, heads_per, HD).transpose(2, 0, 1, 3)

    local_index = jnp.arange(own_count, dtype=jnp.int32)
    own_blocks = (
        local_index // local_blocks * pc_count + pc_place
    ) * local_blocks + local_index % local_blocks
    head_ids = group_place * heads_per + jnp.arange(heads_per, dtype=jnp.int32)
    head_live = head_ids < HEADS
    head_safe = jnp.minimum(head_ids, HEADS - 1)
    own_lists = jnp.take(block_lists[head_safe], own_blocks, axis=1)
    counts = jnp.where(
        head_live[:, None], jnp.take(block_counts[head_safe], own_blocks, axis=1), 0
    )
    visit_count = jnp.max(counts)
    pick_key = jax.vmap(lambda blocks, idx: jnp.take(blocks, idx, axis=0))

    def visit_list(position, running):
        run_max, run_sum, run_acc = running
        picked = lax.dynamic_index_in_dim(own_lists, position, 2, False)
        key_block = pick_key(key_h, picked)
        value_block = pick_key(value_h, picked)
        scores = (
            jnp.einsum(
                "hqad,hqbd->hqab", query_h, key_block, preferred_element_type=jnp.float32
            )
            * score_scale
        )
        live_rows = (position < counts)[:, :, None]
        new_max = jnp.where(live_rows, jnp.maximum(run_max, jnp.max(scores, axis=3)), run_max)
        raised = jnp.where(live_rows[..., None], jnp.exp(scores - new_max[..., None]), 0.0)
        shrink = jnp.exp(run_max - new_max)
        run_sum = run_sum * shrink + jnp.sum(raised, axis=3)
        run_acc = run_acc * shrink[..., None] + jnp.einsum(
            "hqab,hqbd->hqad",
            raised.astype(jnp.bfloat16),
            value_block,
            preferred_element_type=jnp.float32,
        )
        return (new_max, run_sum, run_acc)

    start_state = (
        jnp.full((heads_per, own_count, BLOCK), -1e30, jnp.float32),
        jnp.zeros((heads_per, own_count, BLOCK), jnp.float32),
        jnp.zeros((heads_per, own_count, BLOCK, HD), jnp.float32),
    )
    del max_visits
    run_max, run_sum, run_acc = lax.fori_loop(0, visit_count, visit_list, start_state)
    mixed_out = (run_acc / jnp.where(run_sum > 0.0, run_sum, 1.0)[..., None]).astype(
        jnp.bfloat16
    )
    send_back = mixed_out.transpose(1, 2, 0, 3).reshape(group_count, tok_rows, heads_per * HD)
    returned = lax.all_to_all(send_back, GROUP, 0, 0, tiled=True)
    full = returned.transpose(1, 0, 2).reshape(tok_rows, padded_heads * HD)
    return full[:, : HEADS * HD]


def solution(mesh):
    sizes = dict(zip(mesh.axis_names, mesh.devices.shape))
    pair_count = sizes["pair"]
    pc_count = 2 if pair_count % 2 == 0 else 1
    view = Mesh(
        mesh.devices.reshape(
            sizes["clips"], sizes["seq"], pair_count // pc_count, pc_count
        ),
        ROWS,
    )
    rows = P(ROWS, None)
    return jax.shard_map(
        body,
        mesh=view,
        in_specs=(rows, rows, rows, P(), P()),
        out_specs=rows,
        check_vma=False,
    )
```

```python
import math

import jax
import jax.numpy as jnp
from jax import lax
from jax.experimental import pallas as pl
from jax.experimental.pallas import tpu as pltpu
from jax.sharding import Mesh
from jax.sharding import PartitionSpec as P

HEADS = 40
HD = 128
BLOCK = 128

ROWS = ("clips", "seq", "px", "pc")
GROUP = ("seq", "px")


def body(queries, key_rows, value_rows, block_lists, block_counts):
    seq_count = lax.axis_size("seq")
    px_count = lax.axis_size("px")
    pc_count = lax.axis_size("pc")
    group_count = seq_count * px_count
    group_place = lax.axis_index("seq") * px_count + lax.axis_index("px")
    pc_place = lax.axis_index("pc")
    tok_rows = queries.shape[0]
    local_blocks = tok_rows // BLOCK
    block_total = block_lists.shape[1]
    max_visits = block_lists.shape[2]
    heads_per = -(-HEADS // group_count)
    padded_heads = heads_per * group_count
    score_scale = 1.0 / math.sqrt(HD)

    def to_groups(rows_in):
        widened = rows_in.reshape(tok_rows, HEADS, HD)
        if padded_heads > HEADS:
            widened = jnp.pad(widened, ((0, 0), (0, padded_heads - HEADS), (0, 0)))
        return widened.reshape(tok_rows, group_count, heads_per * HD).transpose(1, 0, 2)

    def exchange(rows_in):
        return lax.all_to_all(to_groups(rows_in), GROUP, 0, 0, tiled=True)

    query_own = exchange(queries)
    key_part = exchange(key_rows)
    value_part = exchange(value_rows)
    key_all = lax.all_gather(key_part, "pc", axis=1)
    value_all = lax.all_gather(value_part, "pc", axis=1)

    own_count = group_count * local_blocks
    local_index = jnp.arange(own_count, dtype=jnp.int32)
    own_blocks = (
        local_index // local_blocks * pc_count + pc_place
    ) * local_blocks + local_index % local_blocks
    head_ids = group_place * heads_per + jnp.arange(heads_per, dtype=jnp.int32)
    head_live = head_ids < HEADS
    head_safe = jnp.minimum(head_ids, HEADS - 1)
    own_lists = jnp.take(block_lists[head_safe], own_blocks, axis=1)
    counts = jnp.where(
        head_live[:, None], jnp.take(block_counts[head_safe], own_blocks, axis=1), 0
    )
    mixed_out = attend(
        own_lists.reshape(-1),
        counts.reshape(-1),
        query_own.reshape(own_count * BLOCK, heads_per * HD),
        key_all.reshape(block_total * BLOCK, heads_per * HD),
        value_all.reshape(block_total * BLOCK, heads_per * HD),
        max_visits,
        score_scale,
    )
    send_back = mixed_out.reshape(group_count, tok_rows, heads_per * HD)
    returned = lax.all_to_all(send_back, GROUP, 0, 0, tiled=True)
    full = returned.transpose(1, 0, 2).reshape(tok_rows, padded_heads * HD)
    return full[:, : HEADS * HD]


def attend(lists, counts, query_rows, key_rows, value_rows, max_visits, score_scale):
    own_rows = query_rows.shape[0]
    all_rows = key_rows.shape[0]
    own_count = own_rows // BLOCK
    heads_per = query_rows.shape[1] // HD

    def kernel(lists_ref, counts_ref, q_ref, k_ref, v_ref, o_ref):
        head = pl.program_id(0)

        def per_block(i, carry):
            slot = head * own_count + i
            visits = counts_ref[slot]
            row = pl.multiple_of(i * BLOCK, BLOCK)
            q = q_ref[pl.ds(row, BLOCK), :]

            def score(j):
                krow = pl.multiple_of(lists_ref[slot * max_visits + j] * BLOCK, BLOCK)
                k = k_ref[pl.ds(krow, BLOCK), :]
                s = lax.dot_general(
                    q, k, (((1,), (1,)), ((), ())), preferred_element_type=jnp.float32
                )
                return s * score_scale, krow

            def max_step(j, m):
                s, _ = score(j)
                return jnp.maximum(m, jnp.max(s, axis=1, keepdims=True))

            m = lax.fori_loop(
                0, visits, max_step, jnp.full((BLOCK, 1), -jnp.inf, jnp.float32)
            )

            def acc_step(j, state):
                total, acc = state
                s, krow = score(j)
                raised = jnp.exp(s - m)
                total = total + jnp.sum(raised, axis=1, keepdims=True)
                acc = acc + jnp.dot(
                    raised.astype(jnp.bfloat16),
                    v_ref[pl.ds(krow, BLOCK), :],
                    preferred_element_type=jnp.float32,
                )
                return total, acc

            total, acc = lax.fori_loop(
                0,
                visits,
                acc_step,
                (jnp.zeros((BLOCK, 1), jnp.float32), jnp.zeros((BLOCK, HD), jnp.float32)),
            )
            total = jnp.where(total > 0.0, total, 1.0)
            o_ref[pl.ds(row, BLOCK), :] = (acc / total).astype(o_ref.dtype)
            return carry

        lax.fori_loop(0, own_count, per_block, 0)

    grid_spec = pltpu.PrefetchScalarGridSpec(
        num_scalar_prefetch=2,
        grid=(heads_per,),
        in_specs=[
            pl.BlockSpec((own_rows, HD), lambda h, *_: (0, h)),
            pl.BlockSpec((all_rows, HD), lambda h, *_: (0, h)),
            pl.BlockSpec((all_rows, HD), lambda h, *_: (0, h)),
        ],
        out_specs=pl.BlockSpec((own_rows, HD), lambda h, *_: (0, h)),
    )
    return pl.pallas_call(
        kernel,
        grid_spec=grid_spec,
        out_shape=jax.ShapeDtypeStruct(query_rows.shape, jnp.bfloat16),
    )(lists, counts, query_rows, key_rows, value_rows)


def solution(mesh):
    sizes = dict(zip(mesh.axis_names, mesh.devices.shape))
    pair_count = sizes["pair"]
    pc_count = 2 if pair_count % 2 == 0 else 1
    view = Mesh(
        mesh.devices.reshape(
            sizes["clips"], sizes["seq"], pair_count // pc_count, pc_count
        ),
        ROWS,
    )
    rows = P(ROWS, None)
    return jax.shard_map(
        body,
        mesh=view,
        in_specs=(rows, rows, rows, P(), P()),
        out_specs=rows,
        check_vma=False,
    )
```

```python
import math

import jax
import jax.numpy as jnp
from jax import lax
from jax.experimental import pallas as pl
from jax.experimental.pallas import tpu as pltpu
from jax.sharding import Mesh
from jax.sharding import PartitionSpec as P

HEADS = 40
HD = 128
BLOCK = 128

ROWS = ("clips", "seq", "px", "pc")
GROUP = ("seq", "px")


def body(queries, key_rows, value_rows, block_lists, block_counts):
    seq_count = lax.axis_size("seq")
    px_count = lax.axis_size("px")
    pc_count = lax.axis_size("pc")
    group_count = seq_count * px_count
    group_place = lax.axis_index("seq") * px_count + lax.axis_index("px")
    pc_place = lax.axis_index("pc")
    tok_rows = queries.shape[0]
    local_blocks = tok_rows // BLOCK
    block_total = block_lists.shape[1]
    max_visits = block_lists.shape[2]
    heads_per = -(-HEADS // group_count)
    padded_heads = heads_per * group_count
    score_scale = 1.0 / math.sqrt(HD)

    def to_groups(rows_in):
        widened = rows_in.reshape(tok_rows, HEADS, HD)
        if padded_heads > HEADS:
            widened = jnp.pad(widened, ((0, 0), (0, padded_heads - HEADS), (0, 0)))
        return widened.reshape(tok_rows, group_count, heads_per * HD).transpose(1, 0, 2)

    def exchange(rows_in):
        return lax.all_to_all(to_groups(rows_in), GROUP, 0, 0, tiled=True)

    query_own = exchange(queries)
    key_part = exchange(key_rows)
    value_part = exchange(value_rows)
    key_all = lax.all_gather(key_part, "pc", axis=1)
    value_all = lax.all_gather(value_part, "pc", axis=1)

    own_count = group_count * local_blocks
    local_index = jnp.arange(own_count, dtype=jnp.int32)
    own_blocks = (
        local_index // local_blocks * pc_count + pc_place
    ) * local_blocks + local_index % local_blocks
    head_ids = group_place * heads_per + jnp.arange(heads_per, dtype=jnp.int32)
    head_live = head_ids < HEADS
    head_safe = jnp.minimum(head_ids, HEADS - 1)
    own_lists = jnp.take(block_lists[head_safe], own_blocks, axis=1)
    counts = jnp.where(
        head_live[:, None], jnp.take(block_counts[head_safe], own_blocks, axis=1), 0
    )
    mixed_out = attend(
        own_lists.reshape(-1),
        counts.reshape(-1),
        query_own.reshape(own_count * BLOCK, heads_per * HD),
        key_all.reshape(block_total * BLOCK, heads_per * HD),
        value_all.reshape(block_total * BLOCK, heads_per * HD),
        max_visits,
        score_scale,
    )
    send_back = mixed_out.reshape(group_count, tok_rows, heads_per * HD)
    returned = lax.all_to_all(send_back, GROUP, 0, 0, tiled=True)
    full = returned.transpose(1, 0, 2).reshape(tok_rows, padded_heads * HD)
    return full[:, : HEADS * HD]


def attend(lists, counts, query_rows, key_rows, value_rows, max_visits, score_scale):
    own_rows = query_rows.shape[0]
    all_rows = key_rows.shape[0]
    own_count = own_rows // BLOCK
    heads_per = query_rows.shape[1] // HD
    kv_blocks = all_rows // BLOCK

    def kernel(lists_ref, counts_ref, q_ref, k_ref, v_ref, o_ref):
        head = pl.program_id(0)

        def per_block(i, carry):
            slot = head * own_count + i
            visits = counts_ref[slot]
            row = pl.multiple_of(i * BLOCK, BLOCK)
            q = q_ref[pl.ds(row, BLOCK), :]
            key_starts = []
            scores = []
            for j in range(max_visits):
                picked = jnp.clip(lists_ref[slot * max_visits + j], 0, kv_blocks - 1)
                krow = pl.multiple_of(picked * BLOCK, BLOCK)
                s = lax.dot_general(
                    q,
                    k_ref[pl.ds(krow, BLOCK), :],
                    (((1,), (1,)), ((), ())),
                    preferred_element_type=jnp.float32,
                )
                key_starts.append(krow)
                scores.append(jnp.where(j < visits, s * score_scale, -jnp.inf))
            peak = scores[0]
            for s in scores[1:]:
                peak = jnp.maximum(peak, s)
            row_max = jnp.max(peak, axis=1, keepdims=True)
            row_max = jnp.where(row_max > -jnp.inf, row_max, 0.0)
            total = jnp.zeros((BLOCK, 1), jnp.float32)
            acc = jnp.zeros((BLOCK, HD), jnp.float32)
            for s, krow in zip(scores, key_starts):
                raised = jnp.exp(s - row_max)
                total = total + jnp.sum(raised, axis=1, keepdims=True)
                acc = acc + jnp.dot(
                    raised.astype(jnp.bfloat16),
                    v_ref[pl.ds(krow, BLOCK), :],
                    preferred_element_type=jnp.float32,
                )
            total = jnp.where(total > 0.0, total, 1.0)
            o_ref[pl.ds(row, BLOCK), :] = (acc / total).astype(o_ref.dtype)
            return carry

        lax.fori_loop(0, own_count, per_block, 0, unroll=min(own_count, 4))

    grid_spec = pltpu.PrefetchScalarGridSpec(
        num_scalar_prefetch=2,
        grid=(heads_per,),
        in_specs=[
            pl.BlockSpec((own_rows, HD), lambda h, *_: (0, h)),
            pl.BlockSpec((all_rows, HD), lambda h, *_: (0, h)),
            pl.BlockSpec((all_rows, HD), lambda h, *_: (0, h)),
        ],
        out_specs=pl.BlockSpec((own_rows, HD), lambda h, *_: (0, h)),
    )
    return pl.pallas_call(
        kernel,
        grid_spec=grid_spec,
        out_shape=jax.ShapeDtypeStruct(query_rows.shape, jnp.bfloat16),
    )(lists, counts, query_rows, key_rows, value_rows)


def solution(mesh):
    sizes = dict(zip(mesh.axis_names, mesh.devices.shape))
    pair_count = sizes["pair"]
    pc_count = 2 if pair_count % 2 == 0 else 1
    view = Mesh(
        mesh.devices.reshape(
            sizes["clips"], sizes["seq"], pair_count // pc_count, pc_count
        ),
        ROWS,
    )
    rows = P(ROWS, None)
    return jax.shard_map(
        body,
        mesh=view,
        in_specs=(rows, rows, rows, P(), P()),
        out_specs=rows,
        check_vma=False,
    )
```

```python
import math

import jax
import jax.numpy as jnp
from jax import lax
from jax.experimental import pallas as pl
from jax.experimental.pallas import tpu as pltpu
from jax.sharding import Mesh
from jax.sharding import PartitionSpec as P

HEADS = 40
HD = 128
BLOCK = 128

ROWS = ("clips", "seq", "px", "pc")
GROUP = ("seq", "px")


def body(queries, key_rows, value_rows, block_lists, block_counts):
    seq_count = lax.axis_size("seq")
    px_count = lax.axis_size("px")
    pc_count = lax.axis_size("pc")
    group_count = seq_count * px_count
    group_place = lax.axis_index("seq") * px_count + lax.axis_index("px")
    pc_place = lax.axis_index("pc")
    tok_rows = queries.shape[0]
    local_blocks = tok_rows // BLOCK
    block_total = block_lists.shape[1]
    max_visits = block_lists.shape[2]
    heads_per = -(-HEADS // group_count)
    padded_heads = heads_per * group_count
    score_scale = 1.0 / math.sqrt(HD)

    def to_groups(rows_in):
        widened = rows_in.reshape(tok_rows, HEADS, HD)
        if padded_heads > HEADS:
            widened = jnp.pad(widened, ((0, 0), (0, padded_heads - HEADS), (0, 0)))
        return widened.reshape(tok_rows, group_count, heads_per * HD).transpose(1, 0, 2)

    def exchange(rows_in):
        return lax.all_to_all(to_groups(rows_in), GROUP, 0, 0, tiled=True)

    query_own = exchange(queries)
    key_part = exchange(key_rows)
    value_part = exchange(value_rows)
    key_all = lax.all_gather(key_part, "pc", axis=1)
    value_all = lax.all_gather(value_part, "pc", axis=1)

    own_count = group_count * local_blocks
    local_index = jnp.arange(own_count, dtype=jnp.int32)
    own_blocks = (
        local_index // local_blocks * pc_count + pc_place
    ) * local_blocks + local_index % local_blocks
    head_ids = group_place * heads_per + jnp.arange(heads_per, dtype=jnp.int32)
    head_live = head_ids < HEADS
    head_safe = jnp.minimum(head_ids, HEADS - 1)
    own_lists = jnp.take(block_lists[head_safe], own_blocks, axis=1)
    counts = jnp.where(
        head_live[:, None], jnp.take(block_counts[head_safe], own_blocks, axis=1), 0
    )
    mixed_out = attend(
        own_lists.reshape(-1),
        counts.reshape(-1),
        query_own.reshape(own_count * BLOCK, heads_per * HD),
        key_all.reshape(block_total * BLOCK, heads_per * HD),
        value_all.reshape(block_total * BLOCK, heads_per * HD),
        max_visits,
        score_scale,
    )
    send_back = mixed_out.reshape(group_count, tok_rows, heads_per * HD)
    returned = lax.all_to_all(send_back, GROUP, 0, 0, tiled=True)
    full = returned.transpose(1, 0, 2).reshape(tok_rows, padded_heads * HD)
    return full[:, : HEADS * HD]


def attend(lists, counts, query_rows, key_rows, value_rows, max_visits, score_scale):
    own_rows = query_rows.shape[0]
    all_rows = key_rows.shape[0]
    own_count = own_rows // BLOCK
    heads_per = query_rows.shape[1] // HD
    kv_blocks = all_rows // BLOCK

    def kernel(lists_ref, counts_ref, q_ref, k_ref, v_ref, o_ref):
        for head in range(heads_per):
            cols = pl.ds(head * HD, HD)

            def per_block(i, carry):
                slot = head * own_count + i
                visits = counts_ref[slot]
                row = pl.multiple_of(i * BLOCK, BLOCK)
                q = q_ref[pl.ds(row, BLOCK), cols]
                key_starts = []
                scores = []
                for j in range(max_visits):
                    picked = jnp.clip(lists_ref[slot * max_visits + j], 0, kv_blocks - 1)
                    krow = pl.multiple_of(picked * BLOCK, BLOCK)
                    s = lax.dot_general(
                        q,
                        k_ref[pl.ds(krow, BLOCK), cols],
                        (((1,), (1,)), ((), ())),
                        preferred_element_type=jnp.float32,
                    )
                    key_starts.append(krow)
                    scores.append(jnp.where(j < visits, s * score_scale, -jnp.inf))
                peak = scores[0]
                for s in scores[1:]:
                    peak = jnp.maximum(peak, s)
                row_max = jnp.max(peak, axis=1, keepdims=True)
                row_max = jnp.where(row_max > -jnp.inf, row_max, 0.0)
                total = jnp.zeros((BLOCK, 1), jnp.float32)
                acc = jnp.zeros((BLOCK, HD), jnp.float32)
                for s, krow in zip(scores, key_starts):
                    raised = jnp.exp(s - row_max)
                    total = total + jnp.sum(raised, axis=1, keepdims=True)
                    acc = acc + jnp.dot(
                        raised.astype(jnp.bfloat16),
                        v_ref[pl.ds(krow, BLOCK), cols],
                        preferred_element_type=jnp.float32,
                    )
                total = jnp.where(total > 0.0, total, 1.0)
                o_ref[pl.ds(row, BLOCK), cols] = (acc / total).astype(o_ref.dtype)
                return carry

            lax.fori_loop(0, own_count, per_block, 0, unroll=min(own_count, 4))

    grid_spec = pltpu.PrefetchScalarGridSpec(
        num_scalar_prefetch=2,
        grid=(1,),
        in_specs=[
            pl.BlockSpec(query_rows.shape, lambda h, *_: (0, 0)),
            pl.BlockSpec(key_rows.shape, lambda h, *_: (0, 0)),
            pl.BlockSpec(value_rows.shape, lambda h, *_: (0, 0)),
        ],
        out_specs=pl.BlockSpec(query_rows.shape, lambda h, *_: (0, 0)),
    )
    return pl.pallas_call(
        kernel,
        grid_spec=grid_spec,
        out_shape=jax.ShapeDtypeStruct(query_rows.shape, jnp.bfloat16),
    )(lists, counts, query_rows, key_rows, value_rows)


def solution(mesh):
    sizes = dict(zip(mesh.axis_names, mesh.devices.shape))
    pair_count = sizes["pair"]
    pc_count = 2 if pair_count % 2 == 0 else 1
    view = Mesh(
        mesh.devices.reshape(
            sizes["clips"], sizes["seq"], pair_count // pc_count, pc_count
        ),
        ROWS,
    )
    rows = P(ROWS, None)
    return jax.shard_map(
        body,
        mesh=view,
        in_specs=(rows, rows, rows, P(), P()),
        out_specs=rows,
        check_vma=False,
    )
```

```python
import math

import jax
import jax.numpy as jnp
from jax import lax
from jax.experimental import pallas as pl
from jax.experimental.pallas import tpu as pltpu
from jax.sharding import Mesh
from jax.sharding import PartitionSpec as P

HEADS = 40
HD = 128
BLOCK = 128

ROWS = ("clips", "seq", "px", "pc")
GROUP = ("seq", "px")


def body(queries, key_rows, value_rows, block_lists, block_counts):
    seq_count = lax.axis_size("seq")
    px_count = lax.axis_size("px")
    pc_count = lax.axis_size("pc")
    group_count = seq_count * px_count
    group_place = lax.axis_index("seq") * px_count + lax.axis_index("px")
    pc_place = lax.axis_index("pc")
    tok_rows = queries.shape[0]
    local_blocks = tok_rows // BLOCK
    block_total = block_lists.shape[1]
    max_visits = block_lists.shape[2]
    heads_per = -(-HEADS // group_count)
    padded_heads = heads_per * group_count
    score_scale = 1.0 / math.sqrt(HD)

    def to_groups(rows_in):
        widened = rows_in.reshape(tok_rows, HEADS, HD)
        if padded_heads > HEADS:
            widened = jnp.pad(widened, ((0, 0), (0, padded_heads - HEADS), (0, 0)))
        return widened.reshape(tok_rows, group_count, heads_per * HD).transpose(1, 0, 2)

    def exchange(rows_in):
        return lax.all_to_all(to_groups(rows_in), GROUP, 0, 0, tiled=True)

    query_own = exchange(queries)
    key_part = exchange(key_rows)
    value_part = exchange(value_rows)
    if pc_count > 1:
        swap = [(c, (c + 1) % pc_count) for c in range(pc_count)]
        key_other = lax.ppermute(key_part, "pc", swap)
        value_other = lax.ppermute(value_part, "pc", swap)
    else:
        key_other, value_other = key_part, value_part

    own_count = group_count * local_blocks
    local_index = jnp.arange(own_count, dtype=jnp.int32)
    own_blocks = (
        local_index // local_blocks * pc_count + pc_place
    ) * local_blocks + local_index % local_blocks
    head_ids = group_place * heads_per + jnp.arange(heads_per, dtype=jnp.int32)
    head_live = head_ids < HEADS
    head_safe = jnp.minimum(head_ids, HEADS - 1)
    own_lists = jnp.take(block_lists[head_safe], own_blocks, axis=1)
    source_pc = own_lists // local_blocks % pc_count
    row_block = own_lists // local_blocks // pc_count * local_blocks + own_lists % local_blocks
    own_lists = jnp.where(source_pc == pc_place, 0, own_count) + row_block
    counts = jnp.where(
        head_live[:, None], jnp.take(block_counts[head_safe], own_blocks, axis=1), 0
    )
    mixed_out = attend(
        own_lists.reshape(-1),
        counts.reshape(-1),
        query_own.reshape(own_count * BLOCK, heads_per * HD),
        key_part.reshape(own_count * BLOCK, heads_per * HD),
        key_other.reshape(own_count * BLOCK, heads_per * HD),
        value_part.reshape(own_count * BLOCK, heads_per * HD),
        value_other.reshape(own_count * BLOCK, heads_per * HD),
        max_visits,
        score_scale,
    )
    send_back = mixed_out.reshape(group_count, tok_rows, heads_per * HD)
    returned = lax.all_to_all(send_back, GROUP, 0, 0, tiled=True)
    full = returned.transpose(1, 0, 2).reshape(tok_rows, padded_heads * HD)
    return full[:, : HEADS * HD]


def attend(
    lists, counts, query_rows, key_mine, key_other, value_mine, value_other, max_visits, score_scale
):
    own_rows = query_rows.shape[0]
    own_count = own_rows // BLOCK
    heads_per = query_rows.shape[1] // HD

    def kernel(lists_ref, counts_ref, q_ref, k_ref, ko_ref, v_ref, vo_ref, o_ref):
        head = pl.program_id(0)

        def per_block(i, carry):
            slot = head * own_count + i
            visits = counts_ref[slot]
            row = pl.multiple_of(i * BLOCK, BLOCK)
            q = q_ref[pl.ds(row, BLOCK), :]
            key_starts = []
            scores = []
            for j in range(max_visits):
                picked = jnp.clip(lists_ref[slot * max_visits + j], 0, 2 * own_count - 1)
                other = picked >= own_count
                krow = pl.multiple_of((picked - jnp.where(other, own_count, 0)) * BLOCK, BLOCK)
                key_block = jnp.where(
                    other, ko_ref[pl.ds(krow, BLOCK), :], k_ref[pl.ds(krow, BLOCK), :]
                )
                s = lax.dot_general(
                    q,
                    key_block,
                    (((1,), (1,)), ((), ())),
                    preferred_element_type=jnp.float32,
                )
                key_starts.append((krow, other))
                scores.append(jnp.where(j < visits, s * score_scale, -jnp.inf))
            peak = scores[0]
            for s in scores[1:]:
                peak = jnp.maximum(peak, s)
            row_max = jnp.max(peak, axis=1, keepdims=True)
            row_max = jnp.where(row_max > -jnp.inf, row_max, 0.0)
            total = jnp.zeros((BLOCK, 1), jnp.float32)
            acc = jnp.zeros((BLOCK, HD), jnp.float32)
            for s, (krow, other) in zip(scores, key_starts):
                raised = jnp.exp(s - row_max)
                total = total + jnp.sum(raised, axis=1, keepdims=True)
                acc = acc + jnp.dot(
                    raised.astype(jnp.bfloat16),
                    jnp.where(
                        other, vo_ref[pl.ds(krow, BLOCK), :], v_ref[pl.ds(krow, BLOCK), :]
                    ),
                    preferred_element_type=jnp.float32,
                )
            total = jnp.where(total > 0.0, total, 1.0)
            o_ref[pl.ds(row, BLOCK), :] = (acc / total).astype(o_ref.dtype)
            return carry

        lax.fori_loop(0, own_count, per_block, 0, unroll=min(own_count, 4))

    grid_spec = pltpu.PrefetchScalarGridSpec(
        num_scalar_prefetch=2,
        grid=(heads_per,),
        in_specs=[
            pl.BlockSpec((own_rows, HD), lambda h, *_: (0, h)),
            pl.BlockSpec((own_rows, HD), lambda h, *_: (0, h)),
            pl.BlockSpec((own_rows, HD), lambda h, *_: (0, h)),
            pl.BlockSpec((own_rows, HD), lambda h, *_: (0, h)),
            pl.BlockSpec((own_rows, HD), lambda h, *_: (0, h)),
        ],
        out_specs=pl.BlockSpec((own_rows, HD), lambda h, *_: (0, h)),
    )
    return pl.pallas_call(
        kernel,
        grid_spec=grid_spec,
        out_shape=jax.ShapeDtypeStruct(query_rows.shape, jnp.bfloat16),
    )(lists, counts, query_rows, key_mine, key_other, value_mine, value_other)


def solution(mesh):
    sizes = dict(zip(mesh.axis_names, mesh.devices.shape))
    pair_count = sizes["pair"]
    pc_count = 2 if pair_count % 2 == 0 else 1
    view = Mesh(
        mesh.devices.reshape(
            sizes["clips"], sizes["seq"], pair_count // pc_count, pc_count
        ),
        ROWS,
    )
    rows = P(ROWS, None)
    return jax.shard_map(
        body,
        mesh=view,
        in_specs=(rows, rows, rows, P(), P()),
        out_specs=rows,
        check_vma=False,
    )
```

```python
import math

import jax
import jax.numpy as jnp
from jax import lax
from jax.experimental import pallas as pl
from jax.experimental.pallas import tpu as pltpu
from jax.sharding import Mesh
from jax.sharding import PartitionSpec as P

HEADS = 40
HD = 128
BLOCK = 128

ROWS = ("clips", "seq", "px", "pc")
GROUP = ("seq", "px")


def body(queries, key_rows, value_rows, block_lists, block_counts):
    seq_count = lax.axis_size("seq")
    px_count = lax.axis_size("px")
    pc_count = lax.axis_size("pc")
    group_count = seq_count * px_count
    group_place = lax.axis_index("seq") * px_count + lax.axis_index("px")
    pc_place = lax.axis_index("pc")
    tok_rows = queries.shape[0]
    local_blocks = tok_rows // BLOCK
    block_total = block_lists.shape[1]
    max_visits = block_lists.shape[2]
    heads_per = -(-HEADS // group_count)
    padded_heads = heads_per * group_count
    score_scale = 1.0 / math.sqrt(HD)

    def to_groups(rows_in):
        widened = rows_in.reshape(tok_rows, HEADS, HD)
        if padded_heads > HEADS:
            widened = jnp.pad(widened, ((0, 0), (0, padded_heads - HEADS), (0, 0)))
        return widened.reshape(tok_rows, group_count, heads_per * HD).transpose(1, 0, 2)

    def exchange(rows_in):
        return lax.all_to_all(to_groups(rows_in), GROUP, 0, 0, tiled=True)

    pair_mine = lax.all_to_all(
        jnp.stack([to_groups(key_rows), to_groups(value_rows)], axis=1), GROUP, 0, 0, tiled=True
    )
    if pc_count > 1:
        swap = [(c, (c + 1) % pc_count) for c in range(pc_count)]
        pair_other = lax.ppermute(pair_mine, "pc", swap)
    else:
        pair_other = pair_mine
    query_own = exchange(queries)

    own_count = group_count * local_blocks
    local_index = jnp.arange(own_count, dtype=jnp.int32)
    own_blocks = (
        local_index // local_blocks * pc_count + pc_place
    ) * local_blocks + local_index % local_blocks
    head_ids = group_place * heads_per + jnp.arange(heads_per, dtype=jnp.int32)
    head_live = head_ids < HEADS
    head_safe = jnp.minimum(head_ids, HEADS - 1)
    own_lists = jnp.take(block_lists[head_safe], own_blocks, axis=1)
    source_pc = own_lists // local_blocks % pc_count
    row_block = own_lists // local_blocks // pc_count * local_blocks + own_lists % local_blocks
    own_lists = jnp.where(source_pc == pc_place, 0, own_count) + row_block
    counts = jnp.where(
        head_live[:, None], jnp.take(block_counts[head_safe], own_blocks, axis=1), 0
    )
    mixed_out = attend(
        own_lists.reshape(-1),
        counts.reshape(-1),
        query_own.reshape(own_count * BLOCK, heads_per * HD),
        pair_mine,
        pair_other,
        max_visits,
        score_scale,
    )
    send_back = mixed_out.reshape(group_count, tok_rows, heads_per * HD)
    returned = lax.all_to_all(send_back, GROUP, 0, 0, tiled=True)
    full = returned.transpose(1, 0, 2).reshape(tok_rows, padded_heads * HD)
    return full[:, : HEADS * HD]


def attend(lists, counts, query_rows, pair_mine, pair_other, max_visits, score_scale):
    own_rows = query_rows.shape[0]
    own_count = own_rows // BLOCK
    heads_per = query_rows.shape[1] // HD
    group_count, _, tok_rows, _ = pair_mine.shape
    local_blocks = tok_rows // BLOCK

    def kernel(lists_ref, counts_ref, q_ref, mine_ref, other_ref, o_ref):
        head = pl.program_id(0)

        def per_block(i, carry):
            slot = head * own_count + i
            visits = counts_ref[slot]
            row = pl.multiple_of(i * BLOCK, BLOCK)
            q = q_ref[pl.ds(row, BLOCK), :]
            key_starts = []
            scores = []
            for j in range(max_visits):
                picked = jnp.clip(lists_ref[slot * max_visits + j], 0, 2 * own_count - 1)
                other = picked >= own_count
                held = picked - jnp.where(other, own_count, 0)
                source = held // local_blocks
                krow = pl.multiple_of(held % local_blocks * BLOCK, BLOCK)
                key_block = jnp.where(
                    other,
                    other_ref[source, 0, pl.ds(krow, BLOCK), :],
                    mine_ref[source, 0, pl.ds(krow, BLOCK), :],
                )
                s = lax.dot_general(
                    q,
                    key_block,
                    (((1,), (1,)), ((), ())),
                    preferred_element_type=jnp.float32,
                )
                key_starts.append((source, krow, other))
                scores.append(jnp.where(j < visits, s * score_scale, -jnp.inf))
            peak = scores[0]
            for s in scores[1:]:
                peak = jnp.maximum(peak, s)
            row_max = jnp.max(peak, axis=1, keepdims=True)
            row_max = jnp.where(row_max > -jnp.inf, row_max, 0.0)
            total = jnp.zeros((BLOCK, 1), jnp.float32)
            acc = jnp.zeros((BLOCK, HD), jnp.float32)
            for s, (source, krow, other) in zip(scores, key_starts):
                raised = jnp.exp(s - row_max)
                total = total + jnp.sum(raised, axis=1, keepdims=True)
                acc = acc + jnp.dot(
                    raised.astype(jnp.bfloat16),
                    jnp.where(
                        other,
                        other_ref[source, 1, pl.ds(krow, BLOCK), :],
                        mine_ref[source, 1, pl.ds(krow, BLOCK), :],
                    ),
                    preferred_element_type=jnp.float32,
                )
            total = jnp.where(total > 0.0, total, 1.0)
            o_ref[pl.ds(row, BLOCK), :] = (acc / total).astype(o_ref.dtype)
            return carry

        lax.fori_loop(0, own_count, per_block, 0, unroll=min(own_count, 4))

    grid_spec = pltpu.PrefetchScalarGridSpec(
        num_scalar_prefetch=2,
        grid=(heads_per,),
        in_specs=[
            pl.BlockSpec((own_rows, HD), lambda h, *_: (0, h)),
            pl.BlockSpec((group_count, 2, tok_rows, HD), lambda h, *_: (0, 0, 0, h)),
            pl.BlockSpec((group_count, 2, tok_rows, HD), lambda h, *_: (0, 0, 0, h)),
        ],
        out_specs=pl.BlockSpec((own_rows, HD), lambda h, *_: (0, h)),
    )
    return pl.pallas_call(
        kernel,
        grid_spec=grid_spec,
        out_shape=jax.ShapeDtypeStruct(query_rows.shape, jnp.bfloat16),
    )(lists, counts, query_rows, pair_mine, pair_other)


def solution(mesh):
    sizes = dict(zip(mesh.axis_names, mesh.devices.shape))
    pair_count = sizes["pair"]
    pc_count = 2 if pair_count % 2 == 0 else 1
    view = Mesh(
        mesh.devices.reshape(
            sizes["clips"], sizes["seq"], pair_count // pc_count, pc_count
        ),
        ROWS,
    )
    rows = P(ROWS, None)
    return jax.shard_map(
        body,
        mesh=view,
        in_specs=(rows, rows, rows, P(), P()),
        out_specs=rows,
        check_vma=False,
    )
```

```python
import math

import jax
import jax.numpy as jnp
from jax import lax
from jax.experimental import pallas as pl
from jax.experimental.pallas import tpu as pltpu
from jax.sharding import Mesh
from jax.sharding import PartitionSpec as P

HEADS = 40
HD = 128
BLOCK = 128

ROWS = ("clips", "seq", "px", "pc")
GROUP = ("seq", "px")


def body(queries, key_rows, value_rows, block_lists, block_counts):
    seq_count = lax.axis_size("seq")
    px_count = lax.axis_size("px")
    pc_count = lax.axis_size("pc")
    group_count = seq_count * px_count
    group_place = lax.axis_index("seq") * px_count + lax.axis_index("px")
    pc_place = lax.axis_index("pc")
    tok_rows = queries.shape[0]
    local_blocks = tok_rows // BLOCK
    block_total = block_lists.shape[1]
    max_visits = block_lists.shape[2]
    heads_per = -(-HEADS // group_count)
    padded_heads = heads_per * group_count
    score_scale = 1.0 / math.sqrt(HD)

    def to_groups(rows_in):
        widened = rows_in.reshape(tok_rows, HEADS, HD)
        if padded_heads > HEADS:
            widened = jnp.pad(widened, ((0, 0), (0, padded_heads - HEADS), (0, 0)))
        return widened.reshape(tok_rows, group_count, heads_per * HD).transpose(1, 0, 2)

    pair_mine = lax.all_to_all(
        jnp.stack([to_groups(key_rows), to_groups(value_rows)], axis=1), GROUP, 0, 0, tiled=True
    )
    if pc_count > 1:
        swap = [(c, (c + 1) % pc_count) for c in range(pc_count)]
        pair_other = lax.ppermute(pair_mine, "pc", swap)
    else:
        pair_other = pair_mine
    query_groups = to_groups(queries)

    own_count = group_count * local_blocks
    local_index = jnp.arange(own_count, dtype=jnp.int32)
    own_blocks = (
        local_index // local_blocks * pc_count + pc_place
    ) * local_blocks + local_index % local_blocks
    head_ids = group_place * heads_per + jnp.arange(heads_per, dtype=jnp.int32)
    head_live = head_ids < HEADS
    head_safe = jnp.minimum(head_ids, HEADS - 1)
    own_lists = jnp.take(block_lists[head_safe], own_blocks, axis=1)
    source_pc = own_lists // local_blocks % pc_count
    row_block = own_lists // local_blocks // pc_count * local_blocks + own_lists % local_blocks
    own_lists = jnp.where(source_pc == pc_place, 0, own_count) + row_block
    counts = jnp.where(
        head_live[:, None], jnp.take(block_counts[head_safe], own_blocks, axis=1), 0
    )
    split = (heads_per + 1) // 2
    chunks = [(0, split), (split, heads_per)] if heads_per > 1 else [(0, heads_per)]
    pieces = []
    for head_lo, head_hi in chunks:
        width = (head_hi - head_lo) * HD
        query_own = lax.all_to_all(
            query_groups[:, :, head_lo * HD : head_hi * HD], GROUP, 0, 0, tiled=True
        )
        mixed_out = attend(
            own_lists[head_lo:head_hi].reshape(-1),
            counts[head_lo:head_hi].reshape(-1),
            query_own.reshape(own_count * BLOCK, width),
            pair_mine,
            pair_other,
            head_lo,
            max_visits,
            score_scale,
        )
        pieces.append(
            lax.all_to_all(
                mixed_out.reshape(group_count, tok_rows, width), GROUP, 0, 0, tiled=True
            )
        )
    returned = jnp.concatenate(pieces, axis=2)
    full = returned.transpose(1, 0, 2).reshape(tok_rows, padded_heads * HD)
    return full[:, : HEADS * HD]


def attend(lists, counts, query_rows, pair_mine, pair_other, head_lo, max_visits, score_scale):
    own_rows = query_rows.shape[0]
    own_count = own_rows // BLOCK
    heads_per = query_rows.shape[1] // HD
    group_count, _, tok_rows, _ = pair_mine.shape
    local_blocks = tok_rows // BLOCK

    def kernel(lists_ref, counts_ref, q_ref, mine_ref, other_ref, o_ref):
        head = pl.program_id(0)

        def per_block(i, carry):
            slot = head * own_count + i
            visits = counts_ref[slot]
            row = pl.multiple_of(i * BLOCK, BLOCK)
            q = q_ref[pl.ds(row, BLOCK), :]
            key_starts = []
            scores = []
            for j in range(max_visits):
                picked = jnp.clip(lists_ref[slot * max_visits + j], 0, 2 * own_count - 1)
                other = picked >= own_count
                held = picked - jnp.where(other, own_count, 0)
                source = held // local_blocks
                krow = pl.multiple_of(held % local_blocks * BLOCK, BLOCK)
                key_block = jnp.where(
                    other,
                    other_ref[source, 0, pl.ds(krow, BLOCK), :],
                    mine_ref[source, 0, pl.ds(krow, BLOCK), :],
                )
                s = lax.dot_general(
                    q,
                    key_block,
                    (((1,), (1,)), ((), ())),
                    preferred_element_type=jnp.float32,
                )
                key_starts.append((source, krow, other))
                scores.append(jnp.where(j < visits, s * score_scale, -jnp.inf))
            peak = scores[0]
            for s in scores[1:]:
                peak = jnp.maximum(peak, s)
            row_max = jnp.max(peak, axis=1, keepdims=True)
            row_max = jnp.where(row_max > -jnp.inf, row_max, 0.0)
            total = jnp.zeros((BLOCK, 1), jnp.float32)
            acc = jnp.zeros((BLOCK, HD), jnp.float32)
            for s, (source, krow, other) in zip(scores, key_starts):
                raised = jnp.exp(s - row_max)
                total = total + jnp.sum(raised, axis=1, keepdims=True)
                acc = acc + jnp.dot(
                    raised.astype(jnp.bfloat16),
                    jnp.where(
                        other,
                        other_ref[source, 1, pl.ds(krow, BLOCK), :],
                        mine_ref[source, 1, pl.ds(krow, BLOCK), :],
                    ),
                    preferred_element_type=jnp.float32,
                )
            total = jnp.where(total > 0.0, total, 1.0)
            o_ref[pl.ds(row, BLOCK), :] = (acc / total).astype(o_ref.dtype)
            return carry

        lax.fori_loop(0, own_count, per_block, 0, unroll=min(own_count, 4))

    grid_spec = pltpu.PrefetchScalarGridSpec(
        num_scalar_prefetch=2,
        grid=(heads_per,),
        in_specs=[
            pl.BlockSpec((own_rows, HD), lambda h, *_: (0, h)),
            pl.BlockSpec((group_count, 2, tok_rows, HD), lambda h, *_: (0, 0, 0, h + head_lo)),
            pl.BlockSpec((group_count, 2, tok_rows, HD), lambda h, *_: (0, 0, 0, h + head_lo)),
        ],
        out_specs=pl.BlockSpec((own_rows, HD), lambda h, *_: (0, h)),
    )
    return pl.pallas_call(
        kernel,
        grid_spec=grid_spec,
        out_shape=jax.ShapeDtypeStruct(query_rows.shape, jnp.bfloat16),
    )(lists, counts, query_rows, pair_mine, pair_other)


def solution(mesh):
    sizes = dict(zip(mesh.axis_names, mesh.devices.shape))
    pair_count = sizes["pair"]
    pc_count = 2 if pair_count % 2 == 0 else 1
    view = Mesh(
        mesh.devices.reshape(
            sizes["clips"], sizes["seq"], pair_count // pc_count, pc_count
        ),
        ROWS,
    )
    rows = P(ROWS, None)
    return jax.shard_map(
        body,
        mesh=view,
        in_specs=(rows, rows, rows, P(), P()),
        out_specs=rows,
        check_vma=False,
    )
```

```python
import math

import jax
import jax.numpy as jnp
from jax import lax
from jax.experimental import pallas as pl
from jax.experimental.pallas import tpu as pltpu
from jax.sharding import Mesh
from jax.sharding import PartitionSpec as P

HEADS = 40
HD = 128
BLOCK = 128

ROWS = ("clips", "seq", "px", "pc")
GROUP = ("seq", "px")


def body(queries, key_rows, value_rows, block_lists, block_counts):
    seq_count = lax.axis_size("seq")
    px_count = lax.axis_size("px")
    pc_count = lax.axis_size("pc")
    group_count = seq_count * px_count
    group_place = lax.axis_index("seq") * px_count + lax.axis_index("px")
    pc_place = lax.axis_index("pc")
    tok_rows = queries.shape[0]
    local_blocks = tok_rows // BLOCK
    block_total = block_lists.shape[1]
    max_visits = block_lists.shape[2]
    heads_per = -(-HEADS // group_count)
    padded_heads = heads_per * group_count
    score_scale = 1.0 / math.sqrt(HD)

    def to_groups(rows_in):
        widened = rows_in.reshape(tok_rows, HEADS, HD)
        if padded_heads > HEADS:
            widened = jnp.pad(widened, ((0, 0), (0, padded_heads - HEADS), (0, 0)))
        return widened.reshape(tok_rows, group_count, heads_per * HD).transpose(1, 0, 2)

    def exchange(rows_in):
        return lax.all_to_all(to_groups(rows_in), GROUP, 0, 0, tiled=True)

    pair_mine = lax.all_to_all(
        jnp.stack([to_groups(key_rows), to_groups(value_rows)], axis=1), GROUP, 0, 0, tiled=True
    )
    if pc_count > 1:
        swap = [(c, (c + 1) % pc_count) for c in range(pc_count)]
        pair_other = lax.ppermute(pair_mine, "pc", swap)
    else:
        pair_other = pair_mine
    query_own = exchange(queries)

    own_count = group_count * local_blocks
    local_index = jnp.arange(own_count, dtype=jnp.int32)
    own_blocks = (
        local_index // local_blocks * pc_count + pc_place
    ) * local_blocks + local_index % local_blocks
    head_ids = group_place * heads_per + jnp.arange(heads_per, dtype=jnp.int32)
    head_live = head_ids < HEADS
    head_safe = jnp.minimum(head_ids, HEADS - 1)
    own_lists = jnp.take(block_lists[head_safe], own_blocks, axis=1)
    source_pc = own_lists // local_blocks % pc_count
    row_block = own_lists // local_blocks // pc_count * local_blocks + own_lists % local_blocks
    own_lists = jnp.where(source_pc == pc_place, 0, own_count) + row_block
    counts = jnp.where(
        head_live[:, None], jnp.take(block_counts[head_safe], own_blocks, axis=1), 0
    )
    mixed_out = attend(
        own_lists.reshape(-1),
        counts.reshape(-1),
        query_own.reshape(own_count * BLOCK, heads_per * HD),
        pair_mine,
        pair_other,
        max_visits,
        score_scale,
    )
    send_back = mixed_out.reshape(group_count, tok_rows, heads_per * HD)
    returned = lax.all_to_all(send_back, GROUP, 0, 0, tiled=True)
    full = returned.transpose(1, 0, 2).reshape(tok_rows, padded_heads * HD)
    return full[:, : HEADS * HD]


def attend(lists, counts, query_rows, pair_mine, pair_other, max_visits, score_scale):
    own_rows = query_rows.shape[0]
    own_count = own_rows // BLOCK
    heads_per = query_rows.shape[1] // HD
    group_count, _, tok_rows, _ = pair_mine.shape
    local_blocks = tok_rows // BLOCK

    def kernel(lists_ref, counts_ref, q_ref, mine_ref, other_ref, o_ref):
        head = pl.program_id(0)

        def per_block(i, carry):
            slot = head * own_count + i
            visits = counts_ref[slot]
            row = pl.multiple_of(i * BLOCK, BLOCK)
            q = q_ref[pl.ds(row, BLOCK), :]
            key_blocks = []
            value_blocks = []
            for j in range(max_visits):
                picked = jnp.clip(lists_ref[slot * max_visits + j], 0, 2 * own_count - 1)
                other = picked >= own_count
                held = picked - jnp.where(other, own_count, 0)
                source = held // local_blocks
                krow = pl.multiple_of(held % local_blocks * BLOCK, BLOCK)
                key_blocks.append(
                    jnp.where(
                        other,
                        other_ref[source, 0, pl.ds(krow, BLOCK), :],
                        mine_ref[source, 0, pl.ds(krow, BLOCK), :],
                    )
                )
                value_blocks.append(
                    jnp.where(
                        other,
                        other_ref[source, 1, pl.ds(krow, BLOCK), :],
                        mine_ref[source, 1, pl.ds(krow, BLOCK), :],
                    )
                )
            s = lax.dot_general(
                q,
                jnp.concatenate(key_blocks, axis=0),
                (((1,), (1,)), ((), ())),
                preferred_element_type=jnp.float32,
            )
            live = lax.broadcasted_iota(jnp.int32, s.shape, 1) < visits * BLOCK
            s = jnp.where(live, s * score_scale, -jnp.inf)
            row_max = jnp.max(s, axis=1, keepdims=True)
            row_max = jnp.where(row_max > -jnp.inf, row_max, 0.0)
            raised = jnp.exp(s - row_max)
            total = jnp.sum(raised, axis=1, keepdims=True)
            acc = jnp.dot(
                raised.astype(jnp.bfloat16),
                jnp.concatenate(value_blocks, axis=0),
                preferred_element_type=jnp.float32,
            )
            total = jnp.where(total > 0.0, total, 1.0)
            o_ref[pl.ds(row, BLOCK), :] = (acc / total).astype(o_ref.dtype)
            return carry

        lax.fori_loop(0, own_count, per_block, 0, unroll=min(own_count, 8))

    grid_spec = pltpu.PrefetchScalarGridSpec(
        num_scalar_prefetch=2,
        grid=(heads_per,),
        in_specs=[
            pl.BlockSpec((own_rows, HD), lambda h, *_: (0, h)),
            pl.BlockSpec((group_count, 2, tok_rows, HD), lambda h, *_: (0, 0, 0, h)),
            pl.BlockSpec((group_count, 2, tok_rows, HD), lambda h, *_: (0, 0, 0, h)),
        ],
        out_specs=pl.BlockSpec((own_rows, HD), lambda h, *_: (0, h)),
    )
    return pl.pallas_call(
        kernel,
        grid_spec=grid_spec,
        out_shape=jax.ShapeDtypeStruct(query_rows.shape, jnp.bfloat16),
    )(lists, counts, query_rows, pair_mine, pair_other)


def solution(mesh):
    sizes = dict(zip(mesh.axis_names, mesh.devices.shape))
    pair_count = sizes["pair"]
    pc_count = 2 if pair_count % 2 == 0 else 1
    view = Mesh(
        mesh.devices.reshape(
            sizes["clips"], sizes["seq"], pair_count // pc_count, pc_count
        ),
        ROWS,
    )
    rows = P(ROWS, None)
    return jax.shard_map(
        body,
        mesh=view,
        in_specs=(rows, rows, rows, P(), P()),
        out_specs=rows,
        check_vma=False,
    )
```

```python
import math

import jax
import jax.numpy as jnp
from jax import lax
from jax.experimental import pallas as pl
from jax.experimental.pallas import tpu as pltpu
from jax.sharding import Mesh
from jax.sharding import PartitionSpec as P

HEADS = 40
HD = 128
BLOCK = 128

ROWS = ("clips", "seq", "px", "pc")
GROUP = ("seq", "px")


def body(queries, key_rows, value_rows, block_lists, block_counts):
    seq_count = lax.axis_size("seq")
    px_count = lax.axis_size("px")
    pc_count = lax.axis_size("pc")
    group_count = seq_count * px_count
    group_place = lax.axis_index("seq") * px_count + lax.axis_index("px")
    pc_place = lax.axis_index("pc")
    tok_rows = queries.shape[0]
    local_blocks = tok_rows // BLOCK
    block_total = block_lists.shape[1]
    max_visits = block_lists.shape[2]
    heads_per = -(-HEADS // group_count)
    padded_heads = heads_per * group_count
    score_scale = 1.0 / math.sqrt(HD)

    def group_slices(rows_in):
        widened = rows_in
        if padded_heads > HEADS:
            widened = jnp.pad(widened, ((0, 0), (0, (padded_heads - HEADS) * HD)))
        width = heads_per * HD
        return [widened[:, g * width : (g + 1) * width] for g in range(group_count)]

    def to_groups(rows_in):
        return jnp.stack(group_slices(rows_in), axis=0)

    pair_mine = lax.all_to_all(
        jnp.stack(
            [
                jnp.stack([key_g, value_g], axis=0)
                for key_g, value_g in zip(group_slices(key_rows), group_slices(value_rows))
            ],
            axis=0,
        ),
        GROUP,
        0,
        0,
        tiled=True,
    )
    if pc_count > 1:
        swap = [(c, (c + 1) % pc_count) for c in range(pc_count)]
        pair_other = lax.ppermute(pair_mine, "pc", swap)
    else:
        pair_other = pair_mine
    query_own = lax.all_to_all(to_groups(queries), GROUP, 0, 0, tiled=True)

    own_count = group_count * local_blocks
    local_index = jnp.arange(own_count, dtype=jnp.int32)
    own_blocks = (
        local_index // local_blocks * pc_count + pc_place
    ) * local_blocks + local_index % local_blocks
    head_ids = group_place * heads_per + jnp.arange(heads_per, dtype=jnp.int32)
    head_live = head_ids < HEADS
    head_safe = jnp.minimum(head_ids, HEADS - 1)
    own_lists = jnp.take(block_lists[head_safe], own_blocks, axis=1)
    source_pc = own_lists // local_blocks % pc_count
    row_block = own_lists // local_blocks // pc_count * local_blocks + own_lists % local_blocks
    own_lists = jnp.where(source_pc == pc_place, 0, own_count) + row_block
    counts = jnp.where(
        head_live[:, None], jnp.take(block_counts[head_safe], own_blocks, axis=1), 0
    )
    mixed_out = attend(
        own_lists.reshape(-1),
        counts.reshape(-1),
        query_own.reshape(own_count * BLOCK, heads_per * HD),
        pair_mine,
        pair_other,
        max_visits,
        score_scale,
    )
    send_back = mixed_out.reshape(group_count, tok_rows, heads_per * HD)
    returned = lax.all_to_all(send_back, GROUP, 0, 0, tiled=True)
    full = returned.transpose(1, 0, 2).reshape(tok_rows, padded_heads * HD)
    return full[:, : HEADS * HD]


def attend(lists, counts, query_rows, pair_mine, pair_other, max_visits, score_scale):
    own_rows = query_rows.shape[0]
    own_count = own_rows // BLOCK
    heads_per = query_rows.shape[1] // HD
    group_count, _, tok_rows, _ = pair_mine.shape
    local_blocks = tok_rows // BLOCK

    def kernel(lists_ref, counts_ref, q_ref, mine_ref, other_ref, o_ref):
        head = pl.program_id(0)

        def per_block(i, carry):
            slot = head * own_count + i
            visits = counts_ref[slot]
            row = pl.multiple_of(i * BLOCK, BLOCK)
            q = q_ref[pl.ds(row, BLOCK), :]
            key_blocks = []
            value_blocks = []
            for j in range(max_visits):
                picked = jnp.clip(lists_ref[slot * max_visits + j], 0, 2 * own_count - 1)
                other = picked >= own_count
                held = picked - jnp.where(other, own_count, 0)
                source = held // local_blocks
                krow = pl.multiple_of(held % local_blocks * BLOCK, BLOCK)
                key_blocks.append(
                    jnp.where(
                        other,
                        other_ref[source, 0, pl.ds(krow, BLOCK), :],
                        mine_ref[source, 0, pl.ds(krow, BLOCK), :],
                    )
                )
                value_blocks.append(
                    jnp.where(
                        other,
                        other_ref[source, 1, pl.ds(krow, BLOCK), :],
                        mine_ref[source, 1, pl.ds(krow, BLOCK), :],
                    )
                )
            s = lax.dot_general(
                q,
                jnp.concatenate(key_blocks, axis=0),
                (((1,), (1,)), ((), ())),
                preferred_element_type=jnp.float32,
            )
            live = lax.broadcasted_iota(jnp.int32, s.shape, 1) < visits * BLOCK
            s = jnp.where(live, s * score_scale, -jnp.inf)
            row_max = jnp.max(s, axis=1, keepdims=True)
            row_max = jnp.where(row_max > -jnp.inf, row_max, 0.0)
            raised = jnp.exp(s - row_max)
            total = jnp.sum(raised, axis=1, keepdims=True)
            acc = jnp.dot(
                raised.astype(jnp.bfloat16),
                jnp.concatenate(value_blocks, axis=0),
                preferred_element_type=jnp.float32,
            )
            total = jnp.where(total > 0.0, total, 1.0)
            o_ref[pl.ds(row, BLOCK), :] = (acc / total).astype(o_ref.dtype)
            return carry

        lax.fori_loop(0, own_count, per_block, 0, unroll=min(own_count, 8))

    grid_spec = pltpu.PrefetchScalarGridSpec(
        num_scalar_prefetch=2,
        grid=(heads_per,),
        in_specs=[
            pl.BlockSpec((own_rows, HD), lambda h, *_: (0, h)),
            pl.BlockSpec((group_count, 2, tok_rows, HD), lambda h, *_: (0, 0, 0, h)),
            pl.BlockSpec((group_count, 2, tok_rows, HD), lambda h, *_: (0, 0, 0, h)),
        ],
        out_specs=pl.BlockSpec((own_rows, HD), lambda h, *_: (0, h)),
    )
    return pl.pallas_call(
        kernel,
        grid_spec=grid_spec,
        out_shape=jax.ShapeDtypeStruct(query_rows.shape, jnp.bfloat16),
    )(lists, counts, query_rows, pair_mine, pair_other)


def solution(mesh):
    sizes = dict(zip(mesh.axis_names, mesh.devices.shape))
    pair_count = sizes["pair"]
    pc_count = 2 if pair_count % 2 == 0 else 1
    view = Mesh(
        mesh.devices.reshape(
            sizes["clips"], sizes["seq"], pair_count // pc_count, pc_count
        ),
        ROWS,
    )
    rows = P(ROWS, None)
    return jax.shard_map(
        body,
        mesh=view,
        in_specs=(rows, rows, rows, P(), P()),
        out_specs=rows,
        check_vma=False,
    )
```

```python
import math

import jax
import jax.numpy as jnp
from jax import lax
from jax.experimental import pallas as pl
from jax.experimental.pallas import tpu as pltpu
from jax.sharding import Mesh
from jax.sharding import PartitionSpec as P

HEADS = 40
HD = 128
BLOCK = 128

ROWS = ("clips", "seq", "px", "pc")
GROUP = ("seq", "px")


def body(queries, key_rows, value_rows, block_lists, block_counts):
    seq_count = lax.axis_size("seq")
    px_count = lax.axis_size("px")
    pc_count = lax.axis_size("pc")
    group_count = seq_count * px_count
    group_place = lax.axis_index("seq") * px_count + lax.axis_index("px")
    pc_place = lax.axis_index("pc")
    tok_rows = queries.shape[0]
    local_blocks = tok_rows // BLOCK
    block_total = block_lists.shape[1]
    max_visits = block_lists.shape[2]
    heads_per = -(-HEADS // group_count)
    padded_heads = heads_per * group_count
    score_scale = 1.0 / math.sqrt(HD)

    def to_groups(rows_in):
        widened = rows_in.reshape(tok_rows, HEADS, HD)
        if padded_heads > HEADS:
            widened = jnp.pad(widened, ((0, 0), (0, padded_heads - HEADS), (0, 0)))
        return widened.reshape(tok_rows, group_count, heads_per * HD).transpose(1, 0, 2)

    if padded_heads == HEADS:
        pair_groups, query_groups = regroup_in(
            key_rows, value_rows, queries, group_count, heads_per * HD
        )
    else:
        pair_groups = jnp.stack([to_groups(key_rows), to_groups(value_rows)], axis=1)
        query_groups = to_groups(queries)
    pair_mine = lax.all_to_all(pair_groups, GROUP, 0, 0, tiled=True)
    if pc_count > 1:
        swap = [(c, (c + 1) % pc_count) for c in range(pc_count)]
        pair_other = lax.ppermute(pair_mine, "pc", swap)
    else:
        pair_other = pair_mine
    query_own = lax.all_to_all(query_groups, GROUP, 0, 0, tiled=True)

    own_count = group_count * local_blocks
    local_index = jnp.arange(own_count, dtype=jnp.int32)
    own_blocks = (
        local_index // local_blocks * pc_count + pc_place
    ) * local_blocks + local_index % local_blocks
    head_ids = group_place * heads_per + jnp.arange(heads_per, dtype=jnp.int32)
    head_live = head_ids < HEADS
    head_safe = jnp.minimum(head_ids, HEADS - 1)
    own_lists = jnp.take(block_lists[head_safe], own_blocks, axis=1)
    source_pc = own_lists // local_blocks % pc_count
    row_block = own_lists // local_blocks // pc_count * local_blocks + own_lists % local_blocks
    own_lists = jnp.where(source_pc == pc_place, 0, own_count) + row_block
    counts = jnp.where(
        head_live[:, None], jnp.take(block_counts[head_safe], own_blocks, axis=1), 0
    )
    mixed_out = attend(
        own_lists.reshape(-1),
        counts.reshape(-1),
        query_own.reshape(own_count * BLOCK, heads_per * HD),
        pair_mine,
        pair_other,
        max_visits,
        score_scale,
    )
    send_back = mixed_out.reshape(group_count, tok_rows, heads_per * HD)
    returned = lax.all_to_all(send_back, GROUP, 0, 0, tiled=True)
    if padded_heads == HEADS:
        return regroup_out(returned)
    full = returned.transpose(1, 0, 2).reshape(tok_rows, padded_heads * HD)
    return full[:, : HEADS * HD]


def attend(lists, counts, query_rows, pair_mine, pair_other, max_visits, score_scale):
    own_rows = query_rows.shape[0]
    own_count = own_rows // BLOCK
    heads_per = query_rows.shape[1] // HD
    group_count, _, tok_rows, _ = pair_mine.shape
    local_blocks = tok_rows // BLOCK

    def kernel(lists_ref, counts_ref, q_ref, mine_ref, other_ref, o_ref):
        head = pl.program_id(0)

        def per_block(i, carry):
            slot = head * own_count + i
            visits = counts_ref[slot]
            row = pl.multiple_of(i * BLOCK, BLOCK)
            q = q_ref[pl.ds(row, BLOCK), :]
            key_blocks = []
            value_blocks = []
            for j in range(max_visits):
                picked = jnp.clip(lists_ref[slot * max_visits + j], 0, 2 * own_count - 1)
                other = picked >= own_count
                held = picked - jnp.where(other, own_count, 0)
                source = held // local_blocks
                krow = pl.multiple_of(held % local_blocks * BLOCK, BLOCK)
                key_blocks.append(
                    jnp.where(
                        other,
                        other_ref[source, 0, pl.ds(krow, BLOCK), :],
                        mine_ref[source, 0, pl.ds(krow, BLOCK), :],
                    )
                )
                value_blocks.append(
                    jnp.where(
                        other,
                        other_ref[source, 1, pl.ds(krow, BLOCK), :],
                        mine_ref[source, 1, pl.ds(krow, BLOCK), :],
                    )
                )
            s = lax.dot_general(
                q,
                jnp.concatenate(key_blocks, axis=0),
                (((1,), (1,)), ((), ())),
                preferred_element_type=jnp.float32,
            )
            live = lax.broadcasted_iota(jnp.int32, s.shape, 1) < visits * BLOCK
            s = jnp.where(live, s * score_scale, -jnp.inf)
            row_max = jnp.max(s, axis=1, keepdims=True)
            row_max = jnp.where(row_max > -jnp.inf, row_max, 0.0)
            raised = jnp.exp(s - row_max)
            total = jnp.sum(raised, axis=1, keepdims=True)
            acc = jnp.dot(
                raised.astype(jnp.bfloat16),
                jnp.concatenate(value_blocks, axis=0),
                preferred_element_type=jnp.float32,
            )
            total = jnp.where(total > 0.0, total, 1.0)
            o_ref[pl.ds(row, BLOCK), :] = (acc / total).astype(o_ref.dtype)
            return carry

        lax.fori_loop(0, own_count, per_block, 0, unroll=min(own_count, 8))

    grid_spec = pltpu.PrefetchScalarGridSpec(
        num_scalar_prefetch=2,
        grid=(heads_per,),
        in_specs=[
            pl.BlockSpec((own_rows, HD), lambda h, *_: (0, h)),
            pl.BlockSpec((group_count, 2, tok_rows, HD), lambda h, *_: (0, 0, 0, h)),
            pl.BlockSpec((group_count, 2, tok_rows, HD), lambda h, *_: (0, 0, 0, h)),
        ],
        out_specs=pl.BlockSpec((own_rows, HD), lambda h, *_: (0, h)),
    )
    return pl.pallas_call(
        kernel,
        grid_spec=grid_spec,
        out_shape=jax.ShapeDtypeStruct(query_rows.shape, jnp.bfloat16),
    )(lists, counts, query_rows, pair_mine, pair_other)


def regroup_in(key_rows, value_rows, queries, group_count, width):
    tok_rows = queries.shape[0]

    def kernel(k_hbm, v_hbm, q_hbm, pair_out, query_out, sems):
        copies = []
        for g in range(group_count):
            cols = pl.ds(g * width, width)
            routes = ((k_hbm, pair_out.at[g, 0]), (v_hbm, pair_out.at[g, 1]), (q_hbm, query_out.at[g]))
            for n, (src, dst) in enumerate(routes):
                copy = pltpu.make_async_copy(src.at[:, cols], dst, sems.at[3 * g + n])
                copy.start()
                copies.append(copy)
        for copy in copies:
            copy.wait()

    anywhere = pl.BlockSpec(memory_space=pl.ANY)
    return pl.pallas_call(
        kernel,
        out_shape=(
            jax.ShapeDtypeStruct((group_count, 2, tok_rows, width), queries.dtype),
            jax.ShapeDtypeStruct((group_count, tok_rows, width), queries.dtype),
        ),
        in_specs=[anywhere, anywhere, anywhere],
        out_specs=(anywhere, anywhere),
        scratch_shapes=[pltpu.SemaphoreType.DMA((3 * group_count,))],
    )(key_rows, value_rows, queries)


def regroup_out(returned):
    group_count, tok_rows, width = returned.shape

    def kernel(r_hbm, o_hbm, sems):
        copies = []
        for g in range(group_count):
            copy = pltpu.make_async_copy(
                r_hbm.at[g], o_hbm.at[:, pl.ds(g * width, width)], sems.at[g]
            )
            copy.start()
            copies.append(copy)
        for copy in copies:
            copy.wait()

    anywhere = pl.BlockSpec(memory_space=pl.ANY)
    return pl.pallas_call(
        kernel,
        out_shape=jax.ShapeDtypeStruct((tok_rows, group_count * width), returned.dtype),
        in_specs=[anywhere],
        out_specs=anywhere,
        scratch_shapes=[pltpu.SemaphoreType.DMA((group_count,))],
    )(returned)


def solution(mesh):
    sizes = dict(zip(mesh.axis_names, mesh.devices.shape))
    pair_count = sizes["pair"]
    pc_count = 2 if pair_count % 2 == 0 else 1
    view = Mesh(
        mesh.devices.reshape(
            sizes["clips"], sizes["seq"], pair_count // pc_count, pc_count
        ),
        ROWS,
    )
    rows = P(ROWS, None)
    return jax.shard_map(
        body,
        mesh=view,
        in_specs=(rows, rows, rows, P(), P()),
        out_specs=rows,
        check_vma=False,
    )
```

```python
import math

import jax
import jax.numpy as jnp
from jax import lax
from jax.experimental import pallas as pl
from jax.experimental.pallas import tpu as pltpu
from jax.sharding import Mesh
from jax.sharding import PartitionSpec as P

HEADS = 40
HD = 128
BLOCK = 128

ROWS = ("clips", "seq", "px", "pc")
GROUP = ("seq", "px")


def body(queries, key_rows, value_rows, block_lists, block_counts):
    seq_count = lax.axis_size("seq")
    px_count = lax.axis_size("px")
    pc_count = lax.axis_size("pc")
    group_count = seq_count * px_count
    group_place = lax.axis_index("seq") * px_count + lax.axis_index("px")
    pc_place = lax.axis_index("pc")
    tok_rows = queries.shape[0]
    local_blocks = tok_rows // BLOCK
    block_total = block_lists.shape[1]
    max_visits = block_lists.shape[2]
    heads_per = -(-HEADS // group_count)
    padded_heads = heads_per * group_count
    score_scale = 1.0 / math.sqrt(HD)

    def to_groups(rows_in):
        widened = rows_in.reshape(tok_rows, HEADS, HD)
        if padded_heads > HEADS:
            widened = jnp.pad(widened, ((0, 0), (0, padded_heads - HEADS), (0, 0)))
        return widened.reshape(tok_rows, group_count, heads_per * HD).transpose(1, 0, 2)

    if padded_heads == HEADS:
        pair_groups, query_groups = regroup_in(
            key_rows, value_rows, queries, group_count, heads_per * HD
        )
    else:
        pair_groups = jnp.stack([to_groups(key_rows), to_groups(value_rows)], axis=1)
        query_groups = to_groups(queries)
    pair_mine = lax.all_to_all(pair_groups, GROUP, 0, 0, tiled=True)
    if pc_count > 1:
        swap = [(c, (c + 1) % pc_count) for c in range(pc_count)]
        pair_other = lax.ppermute(pair_mine, "pc", swap)
    else:
        pair_other = pair_mine
    query_own = lax.all_to_all(query_groups, GROUP, 0, 0, tiled=True)

    own_count = group_count * local_blocks
    local_index = jnp.arange(own_count, dtype=jnp.int32)
    own_blocks = (
        local_index // local_blocks * pc_count + pc_place
    ) * local_blocks + local_index % local_blocks
    head_ids = group_place * heads_per + jnp.arange(heads_per, dtype=jnp.int32)
    head_live = head_ids < HEADS
    head_safe = jnp.minimum(head_ids, HEADS - 1)
    own_lists = jnp.take(block_lists[head_safe], own_blocks, axis=1)
    source_pc = own_lists // local_blocks % pc_count
    row_block = own_lists // local_blocks // pc_count * local_blocks + own_lists % local_blocks
    own_lists = jnp.where(source_pc == pc_place, 0, own_count) + row_block
    counts = jnp.where(
        head_live[:, None], jnp.take(block_counts[head_safe], own_blocks, axis=1), 0
    )
    mixed_out = attend(
        own_lists.reshape(-1),
        counts.reshape(-1),
        query_own.reshape(own_count * BLOCK, heads_per * HD),
        pair_mine,
        pair_other,
        max_visits,
        score_scale,
    )
    send_back = mixed_out.reshape(group_count, tok_rows, heads_per * HD)
    returned = lax.all_to_all(send_back, GROUP, 0, 0, tiled=True)
    full = returned.transpose(1, 0, 2).reshape(tok_rows, padded_heads * HD)
    return full[:, : HEADS * HD]


def attend(lists, counts, query_rows, pair_mine, pair_other, max_visits, score_scale):
    own_rows = query_rows.shape[0]
    own_count = own_rows // BLOCK
    heads_per = query_rows.shape[1] // HD
    group_count, _, tok_rows, _ = pair_mine.shape
    local_blocks = tok_rows // BLOCK

    def kernel(lists_ref, counts_ref, q_ref, mine_ref, other_ref, o_ref):
        head = pl.program_id(0)

        def per_block(i, carry):
            slot = head * own_count + i
            visits = counts_ref[slot]
            row = pl.multiple_of(i * BLOCK, BLOCK)
            q = q_ref[pl.ds(row, BLOCK), :]
            key_blocks = []
            value_blocks = []
            for j in range(max_visits):
                picked = jnp.clip(lists_ref[slot * max_visits + j], 0, 2 * own_count - 1)
                other = picked >= own_count
                held = picked - jnp.where(other, own_count, 0)
                source = held // local_blocks
                krow = pl.multiple_of(held % local_blocks * BLOCK, BLOCK)
                key_blocks.append(
                    jnp.where(
                        other,
                        other_ref[source, 0, pl.ds(krow, BLOCK), :],
                        mine_ref[source, 0, pl.ds(krow, BLOCK), :],
                    )
                )
                value_blocks.append(
                    jnp.where(
                        other,
                        other_ref[source, 1, pl.ds(krow, BLOCK), :],
                        mine_ref[source, 1, pl.ds(krow, BLOCK), :],
                    )
                )
            s = lax.dot_general(
                q,
                jnp.concatenate(key_blocks, axis=0),
                (((1,), (1,)), ((), ())),
                preferred_element_type=jnp.float32,
            )
            live = lax.broadcasted_iota(jnp.int32, s.shape, 1) < visits * BLOCK
            s = jnp.where(live, s * score_scale, -jnp.inf)
            row_max = jnp.max(s, axis=1, keepdims=True)
            row_max = jnp.where(row_max > -jnp.inf, row_max, 0.0)
            raised = jnp.exp(s - row_max)
            total = jnp.sum(raised, axis=1, keepdims=True)
            acc = jnp.dot(
                raised.astype(jnp.bfloat16),
                jnp.concatenate(value_blocks, axis=0),
                preferred_element_type=jnp.float32,
            )
            total = jnp.where(total > 0.0, total, 1.0)
            o_ref[pl.ds(row, BLOCK), :] = (acc / total).astype(o_ref.dtype)
            return carry

        lax.fori_loop(0, own_count, per_block, 0, unroll=min(own_count, 8))

    grid_spec = pltpu.PrefetchScalarGridSpec(
        num_scalar_prefetch=2,
        grid=(heads_per,),
        in_specs=[
            pl.BlockSpec((own_rows, HD), lambda h, *_: (0, h)),
            pl.BlockSpec((group_count, 2, tok_rows, HD), lambda h, *_: (0, 0, 0, h)),
            pl.BlockSpec((group_count, 2, tok_rows, HD), lambda h, *_: (0, 0, 0, h)),
        ],
        out_specs=pl.BlockSpec((own_rows, HD), lambda h, *_: (0, h)),
    )
    return pl.pallas_call(
        kernel,
        grid_spec=grid_spec,
        out_shape=jax.ShapeDtypeStruct(query_rows.shape, jnp.bfloat16),
    )(lists, counts, query_rows, pair_mine, pair_other)


def regroup_in(key_rows, value_rows, queries, group_count, width):
    tok_rows = queries.shape[0]

    def kernel(k_ref, v_ref, q_ref, pair_ref, query_ref):
        for g in range(group_count):
            cols = pl.ds(g * width, width)
            pair_ref[g, 0] = k_ref[:, cols]
            pair_ref[g, 1] = v_ref[:, cols]
            query_ref[g] = q_ref[:, cols]

    return pl.pallas_call(
        kernel,
        out_shape=(
            jax.ShapeDtypeStruct((group_count, 2, tok_rows, width), queries.dtype),
            jax.ShapeDtypeStruct((group_count, tok_rows, width), queries.dtype),
        ),
    )(key_rows, value_rows, queries)


def solution(mesh):
    sizes = dict(zip(mesh.axis_names, mesh.devices.shape))
    pair_count = sizes["pair"]
    pc_count = 2 if pair_count % 2 == 0 else 1
    view = Mesh(
        mesh.devices.reshape(
            sizes["clips"], sizes["seq"], pair_count // pc_count, pc_count
        ),
        ROWS,
    )
    rows = P(ROWS, None)
    return jax.shard_map(
        body,
        mesh=view,
        in_specs=(rows, rows, rows, P(), P()),
        out_specs=rows,
        check_vma=False,
    )
```

```python
import math

import jax
import jax.numpy as jnp
from jax import lax
from jax.experimental import pallas as pl
from jax.experimental.pallas import tpu as pltpu
from jax.sharding import Mesh
from jax.sharding import PartitionSpec as P

HEADS = 40
HD = 128
BLOCK = 128

ROWS = ("clips", "seq", "px", "pc")
GROUP = ("seq", "px")


def body(queries, key_rows, value_rows, block_lists, block_counts):
    seq_count = lax.axis_size("seq")
    px_count = lax.axis_size("px")
    pc_count = lax.axis_size("pc")
    group_count = seq_count * px_count
    group_place = lax.axis_index("seq") * px_count + lax.axis_index("px")
    pc_place = lax.axis_index("pc")
    tok_rows = queries.shape[0]
    local_blocks = tok_rows // BLOCK
    block_total = block_lists.shape[1]
    max_visits = block_lists.shape[2]
    heads_per = -(-HEADS // group_count)
    padded_heads = heads_per * group_count
    score_scale = 1.0 / math.sqrt(HD)

    def to_groups(rows_in):
        widened = rows_in.reshape(tok_rows, HEADS, HD)
        if padded_heads > HEADS:
            widened = jnp.pad(widened, ((0, 0), (0, padded_heads - HEADS), (0, 0)))
        return widened.reshape(tok_rows, group_count, heads_per * HD).transpose(1, 0, 2)

    if padded_heads == HEADS:
        pair_groups, query_groups = regroup_in(
            key_rows, value_rows, queries, group_count, heads_per * HD
        )
    else:
        pair_groups = jnp.stack([to_groups(key_rows), to_groups(value_rows)], axis=1)
        query_groups = to_groups(queries)
    pair_mine = lax.all_to_all(pair_groups, GROUP, 0, 0, tiled=True)
    if pc_count > 1:
        swap = [(c, (c + 1) % pc_count) for c in range(pc_count)]
        pair_other = lax.ppermute(pair_mine, "pc", swap)
    else:
        pair_other = pair_mine
    query_own = lax.all_to_all(query_groups, GROUP, 0, 0, tiled=True)

    own_count = group_count * local_blocks
    mixed_out = attend(
        block_lists.reshape(-1),
        block_counts.reshape(-1),
        query_own.reshape(own_count * BLOCK, heads_per * HD),
        pair_mine,
        pair_other,
        block_total,
        max_visits,
        score_scale,
    )
    send_back = mixed_out.reshape(group_count, tok_rows, heads_per * HD)
    returned = lax.all_to_all(send_back, GROUP, 0, 0, tiled=True)
    full = returned.transpose(1, 0, 2).reshape(tok_rows, padded_heads * HD)
    return full[:, : HEADS * HD]


def attend(lists, counts, query_rows, pair_mine, pair_other, block_total, max_visits, score_scale):
    own_rows = query_rows.shape[0]
    own_count = own_rows // BLOCK
    heads_per = query_rows.shape[1] // HD
    group_count, _, tok_rows, _ = pair_mine.shape
    local_blocks = tok_rows // BLOCK

    def kernel(lists_ref, counts_ref, q_ref, mine_ref, other_ref, o_ref):
        px_count = lax.axis_size("px")
        pc_count = lax.axis_size("pc")
        group_place = lax.axis_index("seq") * px_count + lax.axis_index("px")
        pc_place = lax.axis_index("pc")
        head_id = group_place * heads_per + pl.program_id(0)
        head_safe = jnp.minimum(head_id, HEADS - 1)

        def per_block(i, carry):
            query_block = (i // local_blocks * pc_count + pc_place) * local_blocks + i % local_blocks
            slot = head_safe * block_total + query_block
            visits = jnp.where(head_id < HEADS, counts_ref[slot], 0)
            row = pl.multiple_of(i * BLOCK, BLOCK)
            q = q_ref[pl.ds(row, BLOCK), :]
            key_blocks = []
            value_blocks = []
            for j in range(max_visits):
                picked = jnp.clip(lists_ref[slot * max_visits + j], 0, block_total - 1)
                other = picked // local_blocks % pc_count != pc_place
                source = picked // local_blocks // pc_count
                held = source * local_blocks + picked % local_blocks
                krow = pl.multiple_of(held % local_blocks * BLOCK, BLOCK)
                key_blocks.append(
                    jnp.where(
                        other,
                        other_ref[source, 0, pl.ds(krow, BLOCK), :],
                        mine_ref[source, 0, pl.ds(krow, BLOCK), :],
                    )
                )
                value_blocks.append(
                    jnp.where(
                        other,
                        other_ref[source, 1, pl.ds(krow, BLOCK), :],
                        mine_ref[source, 1, pl.ds(krow, BLOCK), :],
                    )
                )
            s = lax.dot_general(
                q,
                jnp.concatenate(key_blocks, axis=0),
                (((1,), (1,)), ((), ())),
                preferred_element_type=jnp.float32,
            )
            live = lax.broadcasted_iota(jnp.int32, s.shape, 1) < visits * BLOCK
            s = jnp.where(live, s * score_scale, -jnp.inf)
            row_max = jnp.max(s, axis=1, keepdims=True)
            row_max = jnp.where(row_max > -jnp.inf, row_max, 0.0)
            raised = jnp.exp(s - row_max)
            total = jnp.sum(raised, axis=1, keepdims=True)
            acc = jnp.dot(
                raised.astype(jnp.bfloat16),
                jnp.concatenate(value_blocks, axis=0),
                preferred_element_type=jnp.float32,
            )
            total = jnp.where(total > 0.0, total, 1.0)
            o_ref[pl.ds(row, BLOCK), :] = (acc / total).astype(o_ref.dtype)
            return carry

        lax.fori_loop(0, own_count, per_block, 0, unroll=min(own_count, 8))

    grid_spec = pltpu.PrefetchScalarGridSpec(
        num_scalar_prefetch=2,
        grid=(heads_per,),
        in_specs=[
            pl.BlockSpec((own_rows, HD), lambda h, *_: (0, h)),
            pl.BlockSpec((group_count, 2, tok_rows, HD), lambda h, *_: (0, 0, 0, h)),
            pl.BlockSpec((group_count, 2, tok_rows, HD), lambda h, *_: (0, 0, 0, h)),
        ],
        out_specs=pl.BlockSpec((own_rows, HD), lambda h, *_: (0, h)),
    )
    return pl.pallas_call(
        kernel,
        grid_spec=grid_spec,
        out_shape=jax.ShapeDtypeStruct(query_rows.shape, jnp.bfloat16),
    )(lists, counts, query_rows, pair_mine, pair_other)


def regroup_in(key_rows, value_rows, queries, group_count, width):
    tok_rows = queries.shape[0]

    def kernel(k_ref, v_ref, q_ref, pair_ref, query_ref):
        for g in range(group_count):
            cols = pl.ds(g * width, width)
            pair_ref[g, 0] = k_ref[:, cols]
            pair_ref[g, 1] = v_ref[:, cols]
            query_ref[g] = q_ref[:, cols]

    return pl.pallas_call(
        kernel,
        out_shape=(
            jax.ShapeDtypeStruct((group_count, 2, tok_rows, width), queries.dtype),
            jax.ShapeDtypeStruct((group_count, tok_rows, width), queries.dtype),
        ),
    )(key_rows, value_rows, queries)


def solution(mesh):
    sizes = dict(zip(mesh.axis_names, mesh.devices.shape))
    pair_count = sizes["pair"]
    pc_count = 2 if pair_count % 2 == 0 else 1
    view = Mesh(
        mesh.devices.reshape(
            sizes["clips"], sizes["seq"], pair_count // pc_count, pc_count
        ),
        ROWS,
    )
    rows = P(ROWS, None)
    return jax.shard_map(
        body,
        mesh=view,
        in_specs=(rows, rows, rows, P(), P()),
        out_specs=rows,
        check_vma=False,
    )
```

```python
import math

import jax
import jax.numpy as jnp
from jax import lax
from jax.experimental import pallas as pl
from jax.experimental.pallas import tpu as pltpu
from jax.sharding import Mesh
from jax.sharding import PartitionSpec as P

HEADS = 40
HD = 128
BLOCK = 128

ROWS = ("clips", "seq", "px", "pc")
GROUP = ("seq", "px")


def body(queries, key_rows, value_rows, block_lists, block_counts):
    seq_count = lax.axis_size("seq")
    px_count = lax.axis_size("px")
    pc_count = lax.axis_size("pc")
    group_count = seq_count * px_count
    group_place = lax.axis_index("seq") * px_count + lax.axis_index("px")
    pc_place = lax.axis_index("pc")
    tok_rows = queries.shape[0]
    local_blocks = tok_rows // BLOCK
    block_total = block_lists.shape[1]
    max_visits = block_lists.shape[2]
    heads_per = -(-HEADS // group_count)
    padded_heads = heads_per * group_count
    score_scale = 1.0 / math.sqrt(HD)

    def to_groups(rows_in):
        widened = rows_in.reshape(tok_rows, HEADS, HD)
        if padded_heads > HEADS:
            widened = jnp.pad(widened, ((0, 0), (0, padded_heads - HEADS), (0, 0)))
        return widened.reshape(tok_rows, group_count, heads_per * HD).transpose(1, 0, 2)

    split = (heads_per + 1) // 2
    chunks = [(0, split), (split, heads_per)] if heads_per > 1 else [(0, heads_per)]
    if padded_heads == HEADS:
        grouped = regroup_in(key_rows, value_rows, queries, group_count, heads_per, chunks)
    else:
        grouped = []
        for head_lo, head_hi in chunks:
            cols = slice(head_lo * HD, head_hi * HD)
            grouped.append(
                (
                    jnp.stack(
                        [to_groups(key_rows)[:, :, cols], to_groups(value_rows)[:, :, cols]],
                        axis=1,
                    ),
                    to_groups(queries)[:, :, cols],
                )
            )
    own_count = group_count * local_blocks
    pieces = []
    for (head_lo, head_hi), (pair_groups, query_groups) in zip(chunks, grouped):
        width = (head_hi - head_lo) * HD
        pair_mine = lax.all_to_all(pair_groups, GROUP, 0, 0, tiled=True)
        if pc_count > 1:
            swap = [(c, (c + 1) % pc_count) for c in range(pc_count)]
            pair_other = lax.ppermute(pair_mine, "pc", swap)
        else:
            pair_other = pair_mine
        query_own = lax.all_to_all(query_groups, GROUP, 0, 0, tiled=True)
        mixed_out = attend(
            block_lists.reshape(-1),
            block_counts.reshape(-1),
            query_own.reshape(own_count * BLOCK, width),
            pair_mine,
            pair_other,
            head_lo,
            heads_per,
            block_total,
            max_visits,
            score_scale,
        )
        pieces.append(
            lax.all_to_all(
                mixed_out.reshape(group_count, tok_rows, width), GROUP, 0, 0, tiled=True
            )
        )
    returned = jnp.concatenate(pieces, axis=2)
    full = returned.transpose(1, 0, 2).reshape(tok_rows, padded_heads * HD)
    return full[:, : HEADS * HD]


def attend(
    lists,
    counts,
    query_rows,
    pair_mine,
    pair_other,
    head_lo,
    heads_all,
    block_total,
    max_visits,
    score_scale,
):
    own_rows = query_rows.shape[0]
    own_count = own_rows // BLOCK
    heads_per = query_rows.shape[1] // HD
    group_count, _, tok_rows, _ = pair_mine.shape
    local_blocks = tok_rows // BLOCK

    def kernel(lists_ref, counts_ref, q_ref, mine_ref, other_ref, o_ref):
        px_count = lax.axis_size("px")
        pc_count = lax.axis_size("pc")
        group_place = lax.axis_index("seq") * px_count + lax.axis_index("px")
        pc_place = lax.axis_index("pc")
        head_id = group_place * heads_all + head_lo + pl.program_id(0)
        head_safe = jnp.minimum(head_id, HEADS - 1)

        def per_block(i, carry):
            query_block = (i // local_blocks * pc_count + pc_place) * local_blocks + i % local_blocks
            slot = head_safe * block_total + query_block
            visits = jnp.where(head_id < HEADS, counts_ref[slot], 0)
            row = pl.multiple_of(i * BLOCK, BLOCK)
            q = q_ref[pl.ds(row, BLOCK), :]
            key_blocks = []
            value_blocks = []
            for j in range(max_visits):
                picked = jnp.clip(lists_ref[slot * max_visits + j], 0, block_total - 1)
                other = picked // local_blocks % pc_count != pc_place
                source = picked // local_blocks // pc_count
                held = source * local_blocks + picked % local_blocks
                krow = pl.multiple_of(held % local_blocks * BLOCK, BLOCK)
                key_blocks.append(
                    jnp.where(
                        other,
                        other_ref[source, 0, pl.ds(krow, BLOCK), :],
                        mine_ref[source, 0, pl.ds(krow, BLOCK), :],
                    )
                )
                value_blocks.append(
                    jnp.where(
                        other,
                        other_ref[source, 1, pl.ds(krow, BLOCK), :],
                        mine_ref[source, 1, pl.ds(krow, BLOCK), :],
                    )
                )
            s = lax.dot_general(
                q,
                jnp.concatenate(key_blocks, axis=0),
                (((1,), (1,)), ((), ())),
                preferred_element_type=jnp.float32,
            )
            live = lax.broadcasted_iota(jnp.int32, s.shape, 1) < visits * BLOCK
            s = jnp.where(live, s * score_scale, -jnp.inf)
            row_max = jnp.max(s, axis=1, keepdims=True)
            row_max = jnp.where(row_max > -jnp.inf, row_max, 0.0)
            raised = jnp.exp(s - row_max)
            total = jnp.sum(raised, axis=1, keepdims=True)
            acc = jnp.dot(
                raised.astype(jnp.bfloat16),
                jnp.concatenate(value_blocks, axis=0),
                preferred_element_type=jnp.float32,
            )
            total = jnp.where(total > 0.0, total, 1.0)
            o_ref[pl.ds(row, BLOCK), :] = (acc / total).astype(o_ref.dtype)
            return carry

        lax.fori_loop(0, own_count, per_block, 0, unroll=min(own_count, 8))

    grid_spec = pltpu.PrefetchScalarGridSpec(
        num_scalar_prefetch=2,
        grid=(heads_per,),
        in_specs=[
            pl.BlockSpec((own_rows, HD), lambda h, *_: (0, h)),
            pl.BlockSpec((group_count, 2, tok_rows, HD), lambda h, *_: (0, 0, 0, h)),
            pl.BlockSpec((group_count, 2, tok_rows, HD), lambda h, *_: (0, 0, 0, h)),
        ],
        out_specs=pl.BlockSpec((own_rows, HD), lambda h, *_: (0, h)),
    )
    return pl.pallas_call(
        kernel,
        grid_spec=grid_spec,
        out_shape=jax.ShapeDtypeStruct(query_rows.shape, jnp.bfloat16),
    )(lists, counts, query_rows, pair_mine, pair_other)


def regroup_in(key_rows, value_rows, queries, group_count, heads_per, chunks):
    tok_rows = queries.shape[0]

    def kernel(k_ref, v_ref, q_ref, *out_refs):
        for n, (head_lo, head_hi) in enumerate(chunks):
            pair_ref, query_ref = out_refs[2 * n], out_refs[2 * n + 1]
            for g in range(group_count):
                cols = pl.ds((g * heads_per + head_lo) * HD, (head_hi - head_lo) * HD)
                pair_ref[g, 0] = k_ref[:, cols]
                pair_ref[g, 1] = v_ref[:, cols]
                query_ref[g] = q_ref[:, cols]

    shapes = []
    for head_lo, head_hi in chunks:
        width = (head_hi - head_lo) * HD
        shapes.append(jax.ShapeDtypeStruct((group_count, 2, tok_rows, width), queries.dtype))
        shapes.append(jax.ShapeDtypeStruct((group_count, tok_rows, width), queries.dtype))
    outs = pl.pallas_call(kernel, out_shape=tuple(shapes))(key_rows, value_rows, queries)
    return [(outs[2 * n], outs[2 * n + 1]) for n in range(len(chunks))]


def solution(mesh):
    sizes = dict(zip(mesh.axis_names, mesh.devices.shape))
    pair_count = sizes["pair"]
    pc_count = 2 if pair_count % 2 == 0 else 1
    view = Mesh(
        mesh.devices.reshape(
            sizes["clips"], sizes["seq"], pair_count // pc_count, pc_count
        ),
        ROWS,
    )
    rows = P(ROWS, None)
    return jax.shard_map(
        body,
        mesh=view,
        in_specs=(rows, rows, rows, P(), P()),
        out_specs=rows,
        check_vma=False,
    )
```

```python
import math

import jax
import jax.numpy as jnp
from jax import lax
from jax.experimental import pallas as pl
from jax.experimental.pallas import tpu as pltpu
from jax.sharding import Mesh
from jax.sharding import PartitionSpec as P

HEADS = 40
HD = 128
BLOCK = 128

ROWS = ("clips", "seq", "px", "pc")
GROUP = ("seq", "px")


def body(queries, key_rows, value_rows, block_lists, block_counts):
    seq_count = lax.axis_size("seq")
    px_count = lax.axis_size("px")
    pc_count = lax.axis_size("pc")
    group_count = seq_count * px_count
    group_place = lax.axis_index("seq") * px_count + lax.axis_index("px")
    pc_place = lax.axis_index("pc")
    tok_rows = queries.shape[0]
    local_blocks = tok_rows // BLOCK
    block_total = block_lists.shape[1]
    max_visits = block_lists.shape[2]
    heads_per = -(-HEADS // group_count)
    padded_heads = heads_per * group_count
    score_scale = 1.0 / math.sqrt(HD)

    def to_groups(rows_in):
        widened = rows_in.reshape(tok_rows, HEADS, HD)
        if padded_heads > HEADS:
            widened = jnp.pad(widened, ((0, 0), (0, padded_heads - HEADS), (0, 0)))
        return widened.reshape(tok_rows, group_count, heads_per * HD).transpose(1, 0, 2)

    if padded_heads == HEADS:
        pair_groups, query_groups = regroup_in(
            key_rows, value_rows, queries, group_count, heads_per * HD
        )
    else:
        pair_groups = jnp.stack([to_groups(key_rows), to_groups(value_rows)], axis=1)
        query_groups = to_groups(queries)
    pair_mine = lax.all_to_all(pair_groups, GROUP, 0, 0, tiled=True)
    if pc_count > 1:
        swap = [(c, (c + 1) % pc_count) for c in range(pc_count)]
        pair_other = lax.ppermute(pair_mine, "pc", swap)
    else:
        pair_other = pair_mine
    query_own = lax.all_to_all(query_groups, GROUP, 0, 0, tiled=True)

    own_count = group_count * local_blocks
    mixed_out = attend(
        block_lists.reshape(-1),
        block_counts.reshape(-1),
        query_own.reshape(own_count * BLOCK, heads_per * HD),
        pair_mine,
        pair_other,
        block_total,
        max_visits,
        score_scale,
    )
    send_back = mixed_out.reshape(group_count, tok_rows, heads_per * HD)
    returned = lax.all_to_all(send_back, GROUP, 0, 0, tiled=True)
    full = returned.transpose(1, 0, 2).reshape(tok_rows, padded_heads * HD)
    return full[:, : HEADS * HD]


def attend(lists, counts, query_rows, pair_mine, pair_other, block_total, max_visits, score_scale):
    own_rows = query_rows.shape[0]
    own_count = own_rows // BLOCK
    heads_per = query_rows.shape[1] // HD
    group_count, _, tok_rows, _ = pair_mine.shape
    local_blocks = tok_rows // BLOCK

    def kernel(lists_ref, counts_ref, q_hbm, mine_hbm, other_hbm, o_ref, q_buf, mine_buf, other_buf, sems):
        px_count = lax.axis_size("px")
        pc_count = lax.axis_size("pc")
        group_place = lax.axis_index("seq") * px_count + lax.axis_index("px")
        pc_place = lax.axis_index("pc")
        loads = []
        for head_local in range(heads_per):
            cols = pl.ds(head_local * HD, HD)
            routes = (
                (q_hbm.at[:, cols], q_buf.at[head_local]),
                (mine_hbm.at[:, :, :, cols], mine_buf.at[head_local]),
                (other_hbm.at[:, :, :, cols], other_buf.at[head_local]),
            )
            head_loads = []
            for n, (src_ref, dst_ref) in enumerate(routes):
                copy = pltpu.make_async_copy(src_ref, dst_ref, sems.at[3 * head_local + n])
                copy.start()
                head_loads.append(copy)
            loads.append(head_loads)

        for head_local in range(heads_per):
            for copy in loads[head_local]:
                copy.wait()
            cols = pl.ds(head_local * HD, HD)
            q_ref = q_buf.at[head_local]
            mine_ref = mine_buf.at[head_local]
            other_ref = other_buf.at[head_local]
            head_id = group_place * heads_per + head_local
            head_safe = jnp.minimum(head_id, HEADS - 1)

            def per_block(i, carry):
                query_block = (
                    i // local_blocks * pc_count + pc_place
                ) * local_blocks + i % local_blocks
                slot = head_safe * block_total + query_block
                visits = jnp.where(head_id < HEADS, counts_ref[slot], 0)
                row = pl.multiple_of(i * BLOCK, BLOCK)
                q = q_ref[pl.ds(row, BLOCK), :]
                key_blocks = []
                value_blocks = []
                for j in range(max_visits):
                    picked = jnp.clip(lists_ref[slot * max_visits + j], 0, block_total - 1)
                    other = picked // local_blocks % pc_count != pc_place
                    source = picked // local_blocks // pc_count
                    krow = pl.multiple_of(picked % local_blocks * BLOCK, BLOCK)
                    key_blocks.append(
                        jnp.where(
                            other,
                            other_ref[source, 0, pl.ds(krow, BLOCK), :],
                            mine_ref[source, 0, pl.ds(krow, BLOCK), :],
                        )
                    )
                    value_blocks.append(
                        jnp.where(
                            other,
                            other_ref[source, 1, pl.ds(krow, BLOCK), :],
                            mine_ref[source, 1, pl.ds(krow, BLOCK), :],
                        )
                    )
                s = lax.dot_general(
                    q,
                    jnp.concatenate(key_blocks, axis=0),
                    (((1,), (1,)), ((), ())),
                    preferred_element_type=jnp.float32,
                )
                live = lax.broadcasted_iota(jnp.int32, s.shape, 1) < visits * BLOCK
                s = jnp.where(live, s * score_scale, -jnp.inf)
                row_max = jnp.max(s, axis=1, keepdims=True)
                row_max = jnp.where(row_max > -jnp.inf, row_max, 0.0)
                raised = jnp.exp(s - row_max)
                total = jnp.sum(raised, axis=1, keepdims=True)
                acc = jnp.dot(
                    raised.astype(jnp.bfloat16),
                    jnp.concatenate(value_blocks, axis=0),
                    preferred_element_type=jnp.float32,
                )
                total = jnp.where(total > 0.0, total, 1.0)
                o_ref[pl.ds(row, BLOCK), cols] = (acc / total).astype(o_ref.dtype)
                return carry

            lax.fori_loop(0, own_count, per_block, 0, unroll=min(own_count, 8))

    anywhere = pl.BlockSpec(memory_space=pl.ANY)
    grid_spec = pltpu.PrefetchScalarGridSpec(
        num_scalar_prefetch=2,
        grid=(1,),
        in_specs=[anywhere, anywhere, anywhere],
        out_specs=pl.BlockSpec(query_rows.shape, lambda h, *_: (0, 0)),
        scratch_shapes=[
            pltpu.VMEM((heads_per, own_rows, HD), query_rows.dtype),
            pltpu.VMEM((heads_per, group_count, 2, tok_rows, HD), pair_mine.dtype),
            pltpu.VMEM((heads_per, group_count, 2, tok_rows, HD), pair_mine.dtype),
            pltpu.SemaphoreType.DMA((3 * heads_per,)),
        ],
    )
    return pl.pallas_call(
        kernel,
        grid_spec=grid_spec,
        out_shape=jax.ShapeDtypeStruct(query_rows.shape, jnp.bfloat16),
    )(lists, counts, query_rows, pair_mine, pair_other)


def regroup_in(key_rows, value_rows, queries, group_count, width):
    tok_rows = queries.shape[0]

    def kernel(k_ref, v_ref, q_ref, pair_ref, query_ref):
        for g in range(group_count):
            cols = pl.ds(g * width, width)
            pair_ref[g, 0] = k_ref[:, cols]
            pair_ref[g, 1] = v_ref[:, cols]
            query_ref[g] = q_ref[:, cols]

    return pl.pallas_call(
        kernel,
        out_shape=(
            jax.ShapeDtypeStruct((group_count, 2, tok_rows, width), queries.dtype),
            jax.ShapeDtypeStruct((group_count, tok_rows, width), queries.dtype),
        ),
    )(key_rows, value_rows, queries)


def solution(mesh):
    sizes = dict(zip(mesh.axis_names, mesh.devices.shape))
    pair_count = sizes["pair"]
    pc_count = 2 if pair_count % 2 == 0 else 1
    view = Mesh(
        mesh.devices.reshape(
            sizes["clips"], sizes["seq"], pair_count // pc_count, pc_count
        ),
        ROWS,
    )
    rows = P(ROWS, None)
    return jax.shard_map(
        body,
        mesh=view,
        in_specs=(rows, rows, rows, P(), P()),
        out_specs=rows,
        check_vma=False,
    )
```

```python
import math

import jax
import jax.numpy as jnp
from jax import lax
from jax.experimental import pallas as pl
from jax.experimental.pallas import tpu as pltpu
from jax.sharding import Mesh
from jax.sharding import PartitionSpec as P

HEADS = 40
HD = 128
BLOCK = 128

ROWS = ("clips", "seq", "px", "pc")
GROUP = ("seq", "px")


def body(queries, key_rows, value_rows, block_lists, block_counts):
    seq_count = lax.axis_size("seq")
    px_count = lax.axis_size("px")
    pc_count = lax.axis_size("pc")
    group_count = seq_count * px_count
    group_place = lax.axis_index("seq") * px_count + lax.axis_index("px")
    pc_place = lax.axis_index("pc")
    tok_rows = queries.shape[0]
    local_blocks = tok_rows // BLOCK
    block_total = block_lists.shape[1]
    max_visits = block_lists.shape[2]
    heads_per = -(-HEADS // group_count)
    padded_heads = heads_per * group_count
    score_scale = 1.0 / math.sqrt(HD)

    def to_groups(rows_in):
        widened = rows_in.reshape(tok_rows, HEADS, HD)
        if padded_heads > HEADS:
            widened = jnp.pad(widened, ((0, 0), (0, padded_heads - HEADS), (0, 0)))
        return widened.reshape(tok_rows, group_count, heads_per * HD).transpose(1, 0, 2)

    if padded_heads == HEADS:
        pair_groups, query_groups = regroup_in(
            key_rows, value_rows, queries, group_count, heads_per * HD
        )
    else:
        pair_groups = jnp.stack([to_groups(key_rows), to_groups(value_rows)], axis=1)
        query_groups = to_groups(queries)
    pair_mine = lax.all_to_all(pair_groups, GROUP, 0, 0, tiled=True)
    if pc_count > 1:
        swap = [(c, (c + 1) % pc_count) for c in range(pc_count)]
        pair_other = lax.ppermute(pair_mine, "pc", swap)
    else:
        pair_other = pair_mine
    query_own = lax.all_to_all(query_groups, GROUP, 0, 0, tiled=True)

    own_count = group_count * local_blocks
    mixed_out = attend(
        block_lists.reshape(-1),
        block_counts.reshape(-1),
        query_own.reshape(own_count * BLOCK, heads_per * HD),
        pair_mine,
        pair_other,
        block_total,
        max_visits,
        score_scale,
    )
    send_back = mixed_out.reshape(group_count, tok_rows, heads_per * HD)
    returned = lax.all_to_all(send_back, GROUP, 0, 0, tiled=True)
    full = returned.transpose(1, 0, 2).reshape(tok_rows, padded_heads * HD)
    return full[:, : HEADS * HD]


def attend(lists, counts, query_rows, pair_mine, pair_other, block_total, max_visits, score_scale):
    own_rows = query_rows.shape[0]
    own_count = own_rows // BLOCK
    heads_per = query_rows.shape[1] // HD
    group_count, _, tok_rows, _ = pair_mine.shape
    local_blocks = tok_rows // BLOCK

    def kernel(lists_ref, counts_ref, q_hbm, mine_hbm, other_hbm, o_ref, q_buf, mine_buf, other_buf, sems):
        px_count = lax.axis_size("px")
        pc_count = lax.axis_size("pc")
        group_place = lax.axis_index("seq") * px_count + lax.axis_index("px")
        pc_place = lax.axis_index("pc")
        loads = []
        for head_local in range(heads_per):
            cols = pl.ds(head_local * HD, HD)
            routes = (
                (q_hbm.at[:, cols], q_buf.at[head_local]),
                (mine_hbm.at[:, :, :, cols], mine_buf.at[head_local]),
                (other_hbm.at[:, :, :, cols], other_buf.at[head_local]),
            )
            head_loads = []
            for n, (src_ref, dst_ref) in enumerate(routes):
                copy = pltpu.make_async_copy(src_ref, dst_ref, sems.at[3 * head_local + n])
                copy.start()
                head_loads.append(copy)
            loads.append(head_loads)

        for head_local in range(heads_per):
            for copy in loads[head_local]:
                copy.wait()
            cols = pl.ds(head_local * HD, HD)
            q_ref = q_buf.at[head_local]
            mine_ref = mine_buf.at[head_local]
            other_ref = other_buf.at[head_local]
            head_id = group_place * heads_per + head_local
            head_safe = jnp.minimum(head_id, HEADS - 1)

            def per_block(i, carry):
                query_block = (
                    i // local_blocks * pc_count + pc_place
                ) * local_blocks + i % local_blocks
                slot = head_safe * block_total + query_block
                visits = jnp.where(head_id < HEADS, counts_ref[slot], 0)
                row = pl.multiple_of(i * BLOCK, BLOCK)
                q = q_ref[pl.ds(row, BLOCK), :]
                key_blocks = []
                value_blocks = []
                for j in range(max_visits):
                    picked = jnp.clip(lists_ref[slot * max_visits + j], 0, block_total - 1)
                    other = picked // local_blocks % pc_count != pc_place
                    source = picked // local_blocks // pc_count
                    krow = pl.multiple_of(picked % local_blocks * BLOCK, BLOCK)
                    key_blocks.append(
                        jnp.where(
                            other,
                            other_ref[source, 0, pl.ds(krow, BLOCK), :],
                            mine_ref[source, 0, pl.ds(krow, BLOCK), :],
                        )
                    )
                    value_blocks.append(
                        jnp.where(
                            other,
                            other_ref[source, 1, pl.ds(krow, BLOCK), :],
                            mine_ref[source, 1, pl.ds(krow, BLOCK), :],
                        )
                    )
                s = lax.dot_general(
                    q,
                    jnp.concatenate(key_blocks, axis=0),
                    (((1,), (1,)), ((), ())),
                    preferred_element_type=jnp.float32,
                )
                live = lax.broadcasted_iota(jnp.int32, s.shape, 1) < visits * BLOCK
                s = jnp.where(live, s * score_scale, -jnp.inf)
                row_max = jnp.max(s, axis=1, keepdims=True)
                row_max = jnp.where(row_max > -jnp.inf, row_max, 0.0)
                raised = jnp.exp(s - row_max)
                total = jnp.sum(raised, axis=1, keepdims=True)
                acc = jnp.dot(
                    raised.astype(jnp.bfloat16),
                    jnp.concatenate(value_blocks, axis=0),
                    preferred_element_type=jnp.float32,
                )
                total = jnp.where(total > 0.0, total, 1.0)
                o_ref[pl.ds(row, BLOCK), cols] = (acc / total).astype(o_ref.dtype)
                return carry

            lax.fori_loop(0, own_count, per_block, 0, unroll=min(own_count, 8))

    anywhere = pl.BlockSpec(memory_space=pl.ANY)
    grid_spec = pltpu.PrefetchScalarGridSpec(
        num_scalar_prefetch=2,
        grid=(1,),
        in_specs=[anywhere, anywhere, anywhere],
        out_specs=pl.BlockSpec(query_rows.shape, lambda h, *_: (0, 0)),
        scratch_shapes=[
            pltpu.VMEM((heads_per, own_rows, HD), query_rows.dtype),
            pltpu.VMEM((heads_per, group_count, 2, tok_rows, HD), pair_mine.dtype),
            pltpu.VMEM((heads_per, group_count, 2, tok_rows, HD), pair_mine.dtype),
            pltpu.SemaphoreType.DMA((3 * heads_per,)),
        ],
    )
    return pl.pallas_call(
        kernel,
        grid_spec=grid_spec,
        out_shape=jax.ShapeDtypeStruct(query_rows.shape, jnp.bfloat16),
    )(lists, counts, query_rows, pair_mine, pair_other)


def regroup_in(key_rows, value_rows, queries, group_count, width):
    tok_rows = queries.shape[0]

    def kernel(k_hbm, v_hbm, q_hbm, pair_hbm, query_hbm, staged, sems):
        loads = []
        for n, src_ref in enumerate((k_hbm, v_hbm, q_hbm)):
            copy = pltpu.make_async_copy(src_ref, staged.at[n], sems.at[n])
            copy.start()
            loads.append(copy)
        stores = []
        for n in range(3):
            loads[n].wait()
            for g in range(group_count):
                dst_ref = query_hbm.at[g] if n == 2 else pair_hbm.at[g, n]
                copy = pltpu.make_async_copy(
                    staged.at[n, :, pl.ds(g * width, width)],
                    dst_ref,
                    sems.at[3 + n * group_count + g],
                )
                copy.start()
                stores.append(copy)
        for copy in stores:
            copy.wait()

    anywhere = pl.BlockSpec(memory_space=pl.ANY)
    return pl.pallas_call(
        kernel,
        out_shape=(
            jax.ShapeDtypeStruct((group_count, 2, tok_rows, width), queries.dtype),
            jax.ShapeDtypeStruct((group_count, tok_rows, width), queries.dtype),
        ),
        in_specs=[anywhere, anywhere, anywhere],
        out_specs=(anywhere, anywhere),
        scratch_shapes=[
            pltpu.VMEM((3,) + queries.shape, queries.dtype),
            pltpu.SemaphoreType.DMA((3 + 3 * group_count,)),
        ],
    )(key_rows, value_rows, queries)


def solution(mesh):
    sizes = dict(zip(mesh.axis_names, mesh.devices.shape))
    pair_count = sizes["pair"]
    pc_count = 2 if pair_count % 2 == 0 else 1
    view = Mesh(
        mesh.devices.reshape(
            sizes["clips"], sizes["seq"], pair_count // pc_count, pc_count
        ),
        ROWS,
    )
    rows = P(ROWS, None)
    return jax.shard_map(
        body,
        mesh=view,
        in_specs=(rows, rows, rows, P(), P()),
        out_specs=rows,
        check_vma=False,
    )
```

```python
import math

import jax
import jax.numpy as jnp
from jax import lax
from jax.experimental import pallas as pl
from jax.experimental.pallas import tpu as pltpu
from jax.sharding import Mesh
from jax.sharding import PartitionSpec as P

HEADS = 40
HD = 128
BLOCK = 128

ROWS = ("clips", "seq", "px", "pc")
GROUP = ("seq", "px")


def body(queries, key_rows, value_rows, block_lists, block_counts):
    seq_count = lax.axis_size("seq")
    px_count = lax.axis_size("px")
    pc_count = lax.axis_size("pc")
    group_count = seq_count * px_count
    group_place = lax.axis_index("seq") * px_count + lax.axis_index("px")
    pc_place = lax.axis_index("pc")
    tok_rows = queries.shape[0]
    local_blocks = tok_rows // BLOCK
    block_total = block_lists.shape[1]
    max_visits = block_lists.shape[2]
    heads_per = -(-HEADS // group_count)
    padded_heads = heads_per * group_count
    score_scale = 1.0 / math.sqrt(HD)

    def to_groups(rows_in):
        widened = rows_in.reshape(tok_rows, HEADS, HD)
        if padded_heads > HEADS:
            widened = jnp.pad(widened, ((0, 0), (0, padded_heads - HEADS), (0, 0)))
        return widened.reshape(tok_rows, group_count, heads_per * HD).transpose(1, 0, 2)

    if padded_heads == HEADS:
        pair_groups, query_groups = regroup_in(
            key_rows, value_rows, queries, group_count, heads_per * HD
        )
    else:
        pair_groups = jnp.stack([to_groups(key_rows), to_groups(value_rows)], axis=1)
        query_groups = to_groups(queries)
    pair_mine = lax.all_to_all(pair_groups, GROUP, 0, 0, tiled=True)
    if pc_count > 1:
        swap = [(c, (c + 1) % pc_count) for c in range(pc_count)]
        pair_other = lax.ppermute(pair_mine, "pc", swap)
    else:
        pair_other = pair_mine
    query_own = lax.all_to_all(query_groups, GROUP, 0, 0, tiled=True)

    own_count = group_count * local_blocks
    mixed_out = attend(
        block_lists.reshape(-1),
        block_counts.reshape(-1),
        query_own.reshape(own_count * BLOCK, heads_per * HD),
        pair_mine,
        pair_other,
        block_total,
        max_visits,
        score_scale,
    )
    send_back = mixed_out.reshape(group_count, tok_rows, heads_per * HD)
    returned = lax.all_to_all(send_back, GROUP, 0, 0, tiled=True)
    full = returned.transpose(1, 0, 2).reshape(tok_rows, padded_heads * HD)
    return full[:, : HEADS * HD]


def attend(lists, counts, query_rows, pair_mine, pair_other, block_total, max_visits, score_scale):
    own_rows = query_rows.shape[0]
    own_count = own_rows // BLOCK
    heads_per = query_rows.shape[1] // HD
    group_count, _, tok_rows, _ = pair_mine.shape
    local_blocks = tok_rows // BLOCK

    def kernel(
        lists_ref, counts_ref, q_hbm, mine_hbm, other_hbm, o_hbm, q_buf, mine_buf, other_buf, o_buf, sems
    ):
        px_count = lax.axis_size("px")
        pc_count = lax.axis_size("pc")
        group_place = lax.axis_index("seq") * px_count + lax.axis_index("px")
        pc_place = lax.axis_index("pc")
        loads = []
        for head_local in range(heads_per):
            cols = pl.ds(head_local * HD, HD)
            routes = (
                (q_hbm.at[:, cols], q_buf.at[head_local]),
                (mine_hbm.at[:, :, :, cols], mine_buf.at[head_local]),
                (other_hbm.at[:, :, :, cols], other_buf.at[head_local]),
            )
            head_loads = []
            for n, (src_ref, dst_ref) in enumerate(routes):
                copy = pltpu.make_async_copy(src_ref, dst_ref, sems.at[3 * head_local + n])
                copy.start()
                head_loads.append(copy)
            loads.append(head_loads)

        stores = []
        for head_local in range(heads_per):
            for copy in loads[head_local]:
                copy.wait()
            cols = pl.ds(head_local * HD, HD)
            o_ref = o_buf.at[head_local]
            q_ref = q_buf.at[head_local]
            mine_ref = mine_buf.at[head_local]
            other_ref = other_buf.at[head_local]
            head_id = group_place * heads_per + head_local
            head_safe = jnp.minimum(head_id, HEADS - 1)

            def per_block(i, carry):
                query_block = (
                    i // local_blocks * pc_count + pc_place
                ) * local_blocks + i % local_blocks
                slot = head_safe * block_total + query_block
                visits = jnp.where(head_id < HEADS, counts_ref[slot], 0)
                row = pl.multiple_of(i * BLOCK, BLOCK)
                q = q_ref[pl.ds(row, BLOCK), :]
                key_blocks = []
                value_blocks = []
                for j in range(max_visits):
                    picked = jnp.clip(lists_ref[slot * max_visits + j], 0, block_total - 1)
                    other = picked // local_blocks % pc_count != pc_place
                    source = picked // local_blocks // pc_count
                    krow = pl.multiple_of(picked % local_blocks * BLOCK, BLOCK)
                    key_blocks.append(
                        jnp.where(
                            other,
                            other_ref[source, 0, pl.ds(krow, BLOCK), :],
                            mine_ref[source, 0, pl.ds(krow, BLOCK), :],
                        )
                    )
                    value_blocks.append(
                        jnp.where(
                            other,
                            other_ref[source, 1, pl.ds(krow, BLOCK), :],
                            mine_ref[source, 1, pl.ds(krow, BLOCK), :],
                        )
                    )
                s = lax.dot_general(
                    q,
                    jnp.concatenate(key_blocks, axis=0),
                    (((1,), (1,)), ((), ())),
                    preferred_element_type=jnp.float32,
                )
                live = lax.broadcasted_iota(jnp.int32, s.shape, 1) < visits * BLOCK
                s = jnp.where(live, s * score_scale, -jnp.inf)
                row_max = jnp.max(s, axis=1, keepdims=True)
                row_max = jnp.where(row_max > -jnp.inf, row_max, 0.0)
                raised = jnp.exp(s - row_max)
                total = jnp.sum(raised, axis=1, keepdims=True)
                acc = jnp.dot(
                    raised.astype(jnp.bfloat16),
                    jnp.concatenate(value_blocks, axis=0),
                    preferred_element_type=jnp.float32,
                )
                total = jnp.where(total > 0.0, total, 1.0)
                o_ref[pl.ds(row, BLOCK), :] = (acc / total).astype(o_ref.dtype)
                return carry

            lax.fori_loop(0, own_count, per_block, 0, unroll=min(own_count, 8))
            store = pltpu.make_async_copy(
                o_buf.at[head_local], o_hbm.at[:, cols], sems.at[3 * heads_per + head_local]
            )
            store.start()
            stores.append(store)
        for store in stores:
            store.wait()

    anywhere = pl.BlockSpec(memory_space=pl.ANY)
    grid_spec = pltpu.PrefetchScalarGridSpec(
        num_scalar_prefetch=2,
        grid=(1,),
        in_specs=[anywhere, anywhere, anywhere],
        out_specs=anywhere,
        scratch_shapes=[
            pltpu.VMEM((heads_per, own_rows, HD), query_rows.dtype),
            pltpu.VMEM((heads_per, group_count, 2, tok_rows, HD), pair_mine.dtype),
            pltpu.VMEM((heads_per, group_count, 2, tok_rows, HD), pair_mine.dtype),
            pltpu.VMEM((heads_per, own_rows, HD), query_rows.dtype),
            pltpu.SemaphoreType.DMA((4 * heads_per,)),
        ],
    )
    return pl.pallas_call(
        kernel,
        grid_spec=grid_spec,
        out_shape=jax.ShapeDtypeStruct(query_rows.shape, jnp.bfloat16),
    )(lists, counts, query_rows, pair_mine, pair_other)


def regroup_in(key_rows, value_rows, queries, group_count, width):
    tok_rows = queries.shape[0]

    def kernel(k_hbm, v_hbm, q_hbm, pair_hbm, query_hbm, staged, sems):
        loads = []
        for n, src_ref in enumerate((k_hbm, v_hbm, q_hbm)):
            copy = pltpu.make_async_copy(src_ref, staged.at[n], sems.at[n])
            copy.start()
            loads.append(copy)
        stores = []
        for n in range(3):
            loads[n].wait()
            for g in range(group_count):
                dst_ref = query_hbm.at[g] if n == 2 else pair_hbm.at[g, n]
                copy = pltpu.make_async_copy(
                    staged.at[n, :, pl.ds(g * width, width)],
                    dst_ref,
                    sems.at[3 + n * group_count + g],
                )
                copy.start()
                stores.append(copy)
        for copy in stores:
            copy.wait()

    anywhere = pl.BlockSpec(memory_space=pl.ANY)
    return pl.pallas_call(
        kernel,
        out_shape=(
            jax.ShapeDtypeStruct((group_count, 2, tok_rows, width), queries.dtype),
            jax.ShapeDtypeStruct((group_count, tok_rows, width), queries.dtype),
        ),
        in_specs=[anywhere, anywhere, anywhere],
        out_specs=(anywhere, anywhere),
        scratch_shapes=[
            pltpu.VMEM((3,) + queries.shape, queries.dtype),
            pltpu.SemaphoreType.DMA((3 + 3 * group_count,)),
        ],
    )(key_rows, value_rows, queries)


def solution(mesh):
    sizes = dict(zip(mesh.axis_names, mesh.devices.shape))
    pair_count = sizes["pair"]
    pc_count = 2 if pair_count % 2 == 0 else 1
    view = Mesh(
        mesh.devices.reshape(
            sizes["clips"], sizes["seq"], pair_count // pc_count, pc_count
        ),
        ROWS,
    )
    rows = P(ROWS, None)
    return jax.shard_map(
        body,
        mesh=view,
        in_specs=(rows, rows, rows, P(), P()),
        out_specs=rows,
        check_vma=False,
    )
```
